32 devices in a mesh: shard: 2 (over core), tensor: 4 (over y, x), section: 4 (over z).
Axes of the slice: x: 2, y: 2, z: 4, core: 2. Of those that a mesh axis runs over, the one named last changes fastest.
Arguments:
- grad_parts: bfloat16 [2, 2304, 2304], P('shard', ('tensor', 'section')), may hold values from -1.5 to 1.5
- moment: float32 [2304, 2304], P('shard', ('tensor', 'section')), may hold values from -6 to 6
- second: float32 [2304, 2304], P('shard', ('tensor', 'section')), may hold values from 0.05 to 2
- stat_left: float32 [2304, 2304], P('shard', ('tensor', 'section')), may hold values from -0.1 to 12
- basis_left: float32 [2304, 2304], P('shard', ('tensor', 'section')), may hold values from -0.2 to 1.5
Outputs:
- update: float32 [2304, 2304], P('shard', ('tensor', 'section'))
- moment_next: float32 [2304, 2304], P('shard', ('tensor', 'section'))
- second_next: float32 [2304, 2304], P('shard', ('tensor', 'section'))
- stat_next: float32 [2304, 2304], P('shard', ('tensor', 'section'))
- basis_next: float32 [2304, 2304], P('shard', ('tensor', 'section'))
The draws below stay inside these ranges and needn't reach their ends.
All inputs are finite; a program needn't handle non-finite values.
Results may differ from the reference program's by a relative error of at most 0.00074.
Values may be sent and summed in bfloat16 or wider, within the bound.
No kernel may reach another device: no remote copies, remote signals or barrier semaphores. Data moves between devices by JAX's collectives and lax.ppermute only.
A program may use at most 128 MiB of HBM per device.

```python
import math
import jax
import jax.numpy as jnp
from jax import lax

D = 2304
NS_ITERS = 2
N_SHARD = 2


def draw_stat_left(key, part):
    noise_key, scale_key = jax.random.split(jax.random.fold_in(key, 11))
    index = jnp.arange(D, dtype=jnp.float32)
    ramp = 1.0 + 2.0 * index / (D - 1)
    noise = 0.017 * jax.random.normal(noise_key, (D, D), jnp.float32)
    level = jnp.exp(jax.random.uniform(scale_key, (D,), jnp.float32, jnp.log(1.5), jnp.log(3.0)))
    noise = jnp.clip(noise, -0.09, 0.09)
    symmetric = 0.5 * (noise + noise.T)
    diagonal_mask = jnp.eye(D, dtype=jnp.float32)
    return symmetric * (1.0 - diagonal_mask) + diagonal_mask * (level * ramp)[:, None]


def draw_basis_left(key, part):
    noise_key = jax.random.fold_in(jax.random.fold_in(key, 23), 0)
    noise = 0.3 * jax.random.normal(noise_key, (D, D), jnp.float32)
    noise = jnp.clip(noise, -1.8, 1.8) / jnp.sqrt(jnp.float32(D))
    return jnp.eye(D, dtype=jnp.float32) + noise


def spiked(result, key, source, target, shards_of, factor):
    owner, partner = [(jnp.arange(result.shape[dim]) // (result.shape[dim] // shards_of)).reshape([-1 if axis == dim else 1 for axis in range(result.ndim)]) for dim in (source, target)]
    chosen = jax.random.permutation(key, shards_of)[partner]
    strong = (owner == chosen) | (owner == (partner + shards_of // 2) % shards_of)
    return jnp.where(strong, factor * result, result)


def steps_of(own_key, extent, shards, low, top_value):
    loudness, own = 1.0, jax.random.fold_in(own_key, 6)
    for position, shards_of in shards:
        heights = jnp.exp(jax.random.uniform(jax.random.fold_in(own, position), (shards_of,), jnp.float32, low / len(shards), top_value / len(shards)))
        loudness = loudness * jnp.repeat(heights, extent[position] // shards_of).reshape([-1 if axis == position else 1 for axis in range(len(extent))])
    return loudness


def bell_draw(stream_key, extent, spread, reach, shards=(), kind=jnp.bfloat16):
    drawn = spread * jax.random.normal(stream_key, extent, jnp.float32)
    if shards:
        drawn = drawn * steps_of(stream_key, extent, shards, -0.22, 0.18)
    return jnp.clip(drawn, -reach, reach).astype(kind)


def heavy_noise(rng, shape, scale, most, cuts, heavy, kind=jnp.bfloat16):
    values = scale * jax.random.normal(rng, shape, jnp.float32)
    if cuts:
        values = values * steps_of(rng, shape, cuts, -0.22, 0.18)
    return jnp.clip(spiked(values, jax.random.fold_in(rng, 3), *heavy), -most, most).astype(kind)


def setup_inputs(seed: int = 0) -> dict:
    seeds = jax.random.split(jax.random.key(seed), 6)
    grad_parts = heavy_noise(seeds[0], (N_SHARD, D, D), 0.25, 1.5, ((0, 2), (1, 16)), (0, 2, 2, 2.0))
    moment = bell_draw(seeds[1], (D, D), 1.0, 6.0, ((0, 2), (1, 16)), jnp.float32)
    second = jnp.clip(jnp.exp(math.log(2.0) - 3.6888794 * jax.random.uniform(seeds[2], (D, D), jnp.float32) ** steps_of(seeds[2], (D, D), ((0, 2), (1, 16)), -0.2, 0.2)), 0.05, 2.0)
    stat_left = draw_stat_left(jax.random.fold_in(seeds[5], 71), 0)
    basis_left = draw_basis_left(jax.random.fold_in(seeds[5], 71), 0)
    return {"grad_parts": grad_parts, "moment": moment, "second": second, "stat_left": stat_left, "basis_left": basis_left}


beta_one = 0.9
beta_two = 0.95
stat_decay = 0.95
adam_eps = 1e-08
first_fix = 1.0 - 0.9 ** 10
second_fix = 1.0 - 0.95 ** 10
shrink = 0.6
norm_eps = 1e-06

def exact_dot(left, right):
    return jnp.dot(left, right, precision=lax.Precision.HIGHEST, preferred_element_type=jnp.float32)

def reference(grad_parts, moment, second, stat_left, basis_left):
    grad = lax.optimization_barrier(jnp.sum(grad_parts, axis=0, dtype=jnp.float32)).astype(jnp.bfloat16).T
    gram = jnp.dot(grad, grad.T, preferred_element_type=jnp.float32)
    stat_next = stat_decay * stat_left + (1.0 - stat_decay) / D * gram
    rotated = exact_dot(basis_left, grad.astype(jnp.float32))
    moment_next = beta_one * moment + (1.0 - beta_one) * rotated
    second_next = beta_two * second + (1.0 - beta_two) * rotated * rotated
    ratio = moment_next / first_fix / (jnp.sqrt(second_next / second_fix) + adam_eps)
    update = exact_dot(basis_left.T, ratio)
    power = exact_dot(basis_left, stat_next)
    total = jnp.sum(power * power)
    iterate = power * (shrink * jnp.sqrt(D / (total + norm_eps)))
    for turn in range(NS_ITERS):
        iterate = 1.5 * iterate - 0.5 * exact_dot(exact_dot(iterate, iterate.T), iterate)
    return (update, moment_next, second_next, stat_next, iterate)
```

```python
import jax
import jax.numpy as jnp
from jax import lax
from jax.sharding import PartitionSpec as P

D = 2304
NS_ITERS = 2


beta_one = 0.9
beta_two = 0.95
stat_decay = 0.95
adam_eps = 1e-08
first_fix = 1.0 - 0.9**10
second_fix = 1.0 - 0.95**10
shrink = 0.6
norm_eps = 1e-06

TS = ("tensor", "section")


def exact_dot(left, right):
    return jnp.dot(left, right, precision=lax.Precision.HIGHEST, preferred_element_type=jnp.float32)


def contract_rows(left, right):
    return lax.dot_general(
        left,
        right,
        (((0,), (0,)), ((), ())),
        precision=lax.Precision.HIGHEST,
        preferred_element_type=jnp.float32,
    )


def make_shards(n_shard, n_section, n_ts):
    rows = D // n_shard
    cols = D // n_ts
    assert rows % cols == 0 or cols % rows == 0

    def block_rows(grad_rows, k):
        start = k * cols
        if cols <= rows:
            piece = lax.dynamic_slice_in_dim(grad_rows, start % rows, cols, axis=0)
            pieces = lax.all_gather(piece, "shard", axis=0, tiled=False)
            return lax.dynamic_index_in_dim(pieces, start // rows, axis=0, keepdims=False)
        full = lax.all_gather(grad_rows, "shard", axis=0, tiled=True)
        return lax.dynamic_slice_in_dim(full, start, cols, axis=0)

    def newton_step(iterate):
        iterate_rows = lax.all_gather(iterate, TS, axis=1, tiled=True)
        z_cols = lax.psum(contract_rows(iterate_rows, iterate), "shard")
        return 1.5 * iterate - 0.5 * exact_dot(iterate_rows, z_cols)

    def shards(grad_parts, moment, second, stat_left, basis_left):
        k = lax.axis_index("tensor") * n_section + lax.axis_index("section")
        partial_value = grad_parts[0].astype(jnp.float32)
        grad_flip = lax.psum_scatter(
            partial_value.astype(jnp.bfloat16), "shard", scatter_dimension=1, tiled=True
        )
        grad = grad_flip.T
        grad_cols = lax.all_gather(grad, "shard", axis=0, tiled=True)
        grad_rows = lax.all_gather(grad, TS, axis=1, tiled=True)
        grad_krows = block_rows(grad_rows, k)
        gram = lax.dot_general(
            grad_rows, grad_krows, (((1,), (1,)), ((), ())), preferred_element_type=jnp.float32
        )
        stat_next = stat_decay * stat_left + (1.0 - stat_decay) / D * gram
        basis_rows = lax.all_gather(basis_left, TS, axis=1, tiled=True)
        rotated = exact_dot(basis_rows, grad_cols.astype(jnp.float32))
        moment_next = beta_one * moment + (1.0 - beta_one) * rotated
        second_next = beta_two * second + (1.0 - beta_two) * rotated * rotated
        ratio = moment_next / first_fix / (jnp.sqrt(second_next / second_fix) + adam_eps)
        update = lax.psum_scatter(contract_rows(basis_rows, ratio), "shard", scatter_dimension=0, tiled=True)
        power = exact_dot(basis_rows, lax.all_gather(stat_next, "shard", axis=0, tiled=True))
        total_sq = lax.psum(jnp.sum(power * power), ("shard", "tensor", "section"))
        scale = shrink * jnp.sqrt(D / (total_sq + norm_eps))
        iterate = power * scale
        for turn in range(NS_ITERS):
            iterate = newton_step(iterate)
        return (update, moment_next, second_next, stat_next, iterate)

    return shards


def solution(mesh):
    n_shard = mesh.shape["shard"]
    n_section = mesh.shape["section"]
    n_ts = mesh.shape["tensor"] * n_section
    in_specs = (
        P("shard", TS, None),
        P("shard", TS),
        P("shard", TS),
        P("shard", TS),
        P("shard", TS),
    )
    out_specs = (
        P("shard", TS),
        P("shard", TS),
        P("shard", TS),
        P("shard", TS),
        P("shard", TS),
    )
    return jax.shard_map(
        make_shards(n_shard, n_section, n_ts), mesh=mesh, in_specs=in_specs, out_specs=out_specs, check_vma=False
    )
```

```python
import jax
import jax.numpy as jnp
from jax import lax
from jax.sharding import PartitionSpec as P

D = 2304
NS_ITERS = 2


beta_one = 0.9
beta_two = 0.95
stat_decay = 0.95
adam_eps = 1e-08
first_fix = 1.0 - 0.9**10
second_fix = 1.0 - 0.95**10
shrink = 0.6
norm_eps = 1e-06

TS = ("tensor", "section")


def exact_dot(left, right):
    return jnp.dot(left, right, precision=lax.Precision.HIGH, preferred_element_type=jnp.float32)


def contract_rows(left, right):
    return lax.dot_general(
        left,
        right,
        (((0,), (0,)), ((), ())),
        precision=lax.Precision.HIGH,
        preferred_element_type=jnp.float32,
    )


def make_shards(n_shard, n_section, n_ts):
    rows = D // n_shard
    cols = D // n_ts
    assert rows % cols == 0 or cols % rows == 0

    def block_rows(grad_rows, k):
        start = k * cols
        if cols <= rows:
            piece = lax.dynamic_slice_in_dim(grad_rows, start % rows, cols, axis=0)
            pieces = lax.all_gather(piece, "shard", axis=0, tiled=False)
            return lax.dynamic_index_in_dim(pieces, start // rows, axis=0, keepdims=False)
        full = lax.all_gather(grad_rows, "shard", axis=0, tiled=True)
        return lax.dynamic_slice_in_dim(full, start, cols, axis=0)

    def newton_step(iterate):
        iterate_rows = lax.all_gather(iterate, TS, axis=1, tiled=True)
        z_cols = lax.psum(contract_rows(iterate_rows, iterate), "shard")
        return 1.5 * iterate - 0.5 * exact_dot(iterate_rows, z_cols)

    def shards(grad_parts, moment, second, stat_left, basis_left):
        k = lax.axis_index("tensor") * n_section + lax.axis_index("section")
        partial_value = grad_parts[0].astype(jnp.float32)
        grad_flip = lax.psum_scatter(
            partial_value.astype(jnp.bfloat16), "shard", scatter_dimension=1, tiled=True
        )
        grad = grad_flip.T
        grad_cols = lax.all_gather(grad, "shard", axis=0, tiled=True)
        grad_rows = lax.all_gather(grad, TS, axis=1, tiled=True)
        grad_krows = block_rows(grad_rows, k)
        gram = lax.dot_general(
            grad_rows, grad_krows, (((1,), (1,)), ((), ())), preferred_element_type=jnp.float32
        )
        stat_next = stat_decay * stat_left + (1.0 - stat_decay) / D * gram
        basis_rows = lax.all_gather(basis_left, TS, axis=1, tiled=True)
        rotated = exact_dot(basis_rows, grad_cols.astype(jnp.float32))
        moment_next = beta_one * moment + (1.0 - beta_one) * rotated
        second_next = beta_two * second + (1.0 - beta_two) * rotated * rotated
        ratio = moment_next / first_fix / (jnp.sqrt(second_next / second_fix) + adam_eps)
        update = lax.psum_scatter(contract_rows(basis_rows, ratio), "shard", scatter_dimension=0, tiled=True)
        power = exact_dot(basis_rows, lax.all_gather(stat_next, "shard", axis=0, tiled=True))
        power_rows = lax.all_gather(power, TS, axis=1, tiled=True)
        power_rows, update = lax.optimization_barrier((power_rows, update))
        z_part = contract_rows(power_rows, power)
        sq_part = jnp.full((8, cols), jnp.sum(power_rows * power_rows), jnp.float32)
        summed = lax.psum(jnp.concatenate([z_part, sq_part], axis=0), "shard")
        total_sq = summed[D, 0]
        scale = shrink * jnp.sqrt(D / (total_sq + norm_eps))
        iterate = (1.5 * scale) * power - (0.5 * scale * scale * scale) * exact_dot(power_rows, summed[:D])
        for turn in range(NS_ITERS - 1):
            iterate = newton_step(iterate)
        return (update, moment_next, second_next, stat_next, iterate)

    return shards


def solution(mesh):
    n_shard = mesh.shape["shard"]
    n_section = mesh.shape["section"]
    n_ts = mesh.shape["tensor"] * n_section
    in_specs = (
        P("shard", TS, None),
        P("shard", TS),
        P("shard", TS),
        P("shard", TS),
        P("shard", TS),
    )
    out_specs = (
        P("shard", TS),
        P("shard", TS),
        P("shard", TS),
        P("shard", TS),
        P("shard", TS),
    )
    return jax.shard_map(
        make_shards(n_shard, n_section, n_ts), mesh=mesh, in_specs=in_specs, out_specs=out_specs, check_vma=False
    )
```

```python
import jax
import jax.numpy as jnp
from jax import lax
from jax.sharding import PartitionSpec as P

D = 2304
NS_ITERS = 2


beta_one = 0.9
beta_two = 0.95
stat_decay = 0.95
adam_eps = 1e-08
first_fix = 1.0 - 0.9**10
second_fix = 1.0 - 0.95**10
shrink = 0.6
norm_eps = 1e-06

TS = ("tensor", "section")
PAD = 8


def exact_dot(left, right):
    return jnp.dot(left, right, precision=lax.Precision.HIGH, preferred_element_type=jnp.float32)


def contract_rows(left, right):
    return lax.dot_general(
        left,
        right,
        (((0,), (0,)), ((), ())),
        precision=lax.Precision.HIGH,
        preferred_element_type=jnp.float32,
    )


def make_shards(n_shard, n_section, n_ts):
    rows = D // n_shard
    cols = D // n_ts
    assert rows % cols == 0 or cols % rows == 0
    pair = n_shard == 2

    def partner(x):
        return lax.ppermute(x, "shard", [(0, 1), (1, 0)])

    def shard_concat(x, c):
        if not pair:
            return lax.all_gather(x, "shard", axis=0, tiled=True)
        other = partner(x)
        first = jnp.where(c == 0, x, other)
        last = jnp.where(c == 0, other, x)
        return jnp.concatenate([first, last], axis=0)

    def shard_sum(x):
        if not pair:
            return lax.psum(x, "shard")
        return x + partner(x)

    def shard_sum_scatter(x, c, axis):
        if not pair:
            return lax.psum_scatter(x, "shard", scatter_dimension=axis, tiled=True)
        size = x.shape[axis] // 2
        mine = lax.dynamic_slice_in_dim(x, c * size, size, axis=axis)
        theirs = lax.dynamic_slice_in_dim(x, (1 - c) * size, size, axis=axis)
        return mine + partner(theirs)

    def block_rows(grad_rows, k, c):
        start = k * cols
        if cols <= rows:
            piece = lax.dynamic_slice_in_dim(grad_rows, start % rows, cols, axis=0)
            owner = start // rows
            if pair:
                return jnp.where(owner == c, piece, partner(piece))
            pieces = lax.all_gather(piece, "shard", axis=0, tiled=False)
            return lax.dynamic_index_in_dim(pieces, owner, axis=0, keepdims=False)
        full = lax.all_gather(grad_rows, "shard", axis=0, tiled=True)
        return lax.dynamic_slice_in_dim(full, start, cols, axis=0)

    def gather_rows(block, extra):
        padded = jnp.concatenate([block, jnp.full((PAD, cols), extra, jnp.float32)], axis=0)
        gathered = lax.all_gather(padded, TS, axis=1, tiled=True)
        return gathered[:rows], gathered[rows, ::cols]

    def newton_step(iterate):
        iterate_rows = lax.all_gather(iterate, TS, axis=1, tiled=True)
        z_cols = shard_sum(contract_rows(iterate_rows, iterate))
        return 1.5 * iterate - 0.5 * exact_dot(iterate_rows, z_cols)

    def shards(grad_parts, moment, second, stat_left, basis_left):
        c = lax.axis_index("shard")
        k = lax.axis_index("tensor") * n_section + lax.axis_index("section")
        part = grad_parts[0]
        if pair:
            mine = lax.dynamic_slice_in_dim(part, c * rows, rows, axis=1)
            theirs = lax.dynamic_slice_in_dim(part, (1 - c) * rows, rows, axis=1)
            grad_flip = (mine.astype(jnp.float32) + partner(theirs).astype(jnp.float32)).astype(jnp.bfloat16)
        else:
            grad_flip = lax.psum_scatter(
                part.astype(jnp.float32).astype(jnp.bfloat16), "shard", scatter_dimension=1, tiled=True
            )
        grad = grad_flip.T
        grad_cols = shard_concat(grad, c)
        grad_rows = lax.all_gather(grad, TS, axis=1, tiled=True)
        grad_krows = block_rows(grad_rows, k, c)
        gram = lax.dot_general(
            grad_rows, grad_krows, (((1,), (1,)), ((), ())), preferred_element_type=jnp.float32
        )
        stat_next = stat_decay * stat_left + (1.0 - stat_decay) / D * gram
        basis_rows = lax.all_gather(basis_left, TS, axis=1, tiled=True)
        power = exact_dot(basis_rows, shard_concat(stat_next, c))
        power, basis_later = lax.optimization_barrier((power, basis_rows))
        rotated = exact_dot(basis_later, grad_cols.astype(jnp.float32))
        moment_next = beta_one * moment + (1.0 - beta_one) * rotated
        second_next = beta_two * second + (1.0 - beta_two) * rotated * rotated
        ratio = moment_next / first_fix / (jnp.sqrt(second_next / second_fix) + adam_eps)
        update = shard_sum_scatter(contract_rows(basis_later, ratio), c, 0)
        power_rows, block_sq = gather_rows(power, jnp.sum(power * power))
        power_rows, update = lax.optimization_barrier((power_rows, update))
        z_part = contract_rows(power_rows, power)
        sq_part = jnp.full((PAD, cols), jnp.sum(block_sq), jnp.float32)
        summed = shard_sum(jnp.concatenate([z_part, sq_part], axis=0))
        total_sq = summed[D, 0]
        scale = shrink * jnp.sqrt(D / (total_sq + norm_eps))
        iterate = (1.5 * scale) * power - (0.5 * scale * scale * scale) * exact_dot(power_rows, summed[:D])
        for turn in range(NS_ITERS - 1):
            iterate = newton_step(iterate)
        return (update, moment_next, second_next, stat_next, iterate)

    return shards


def solution(mesh):
    n_shard = mesh.shape["shard"]
    n_section = mesh.shape["section"]
    n_ts = mesh.shape["tensor"] * n_section
    in_specs = (
        P("shard", TS, None),
        P("shard", TS),
        P("shard", TS),
        P("shard", TS),
        P("shard", TS),
    )
    out_specs = (
        P("shard", TS),
        P("shard", TS),
        P("shard", TS),
        P("shard", TS),
        P("shard", TS),
    )
    return jax.shard_map(
        make_shards(n_shard, n_section, n_ts), mesh=mesh, in_specs=in_specs, out_specs=out_specs, check_vma=False
    )
```

```python
import jax
import jax.numpy as jnp
from jax import lax
from jax.sharding import PartitionSpec as P

D = 2304
NS_ITERS = 2


beta_one = 0.9
beta_two = 0.95
stat_decay = 0.95
adam_eps = 1e-08
first_fix = 1.0 - 0.9**10
second_fix = 1.0 - 0.95**10
shrink = 0.6
norm_eps = 1e-06

TS = ("tensor", "section")
PAD = 8


def exact_dot(left, right):
    return jnp.dot(left, right, precision=lax.Precision.HIGH, preferred_element_type=jnp.float32)


def contract_rows(left, right):
    return lax.dot_general(
        left,
        right,
        (((0,), (0,)), ((), ())),
        precision=lax.Precision.HIGH,
        preferred_element_type=jnp.float32,
    )


def make_shards(n_shard, n_section, n_ts):
    rows = D // n_shard
    cols = D // n_ts
    assert rows % cols == 0 or cols % rows == 0
    pair = n_shard == 2

    def partner(x):
        return lax.ppermute(x, "shard", [(0, 1), (1, 0)])

    def shard_concat(x, c):
        if not pair:
            return lax.all_gather(x, "shard", axis=0, tiled=True)
        other = partner(x)
        first = jnp.where(c == 0, x, other)
        last = jnp.where(c == 0, other, x)
        return jnp.concatenate([first, last], axis=0)

    def shard_sum(x):
        if not pair:
            return lax.psum(x, "shard")
        return x + partner(x)

    def shard_sum_scatter(x, c, axis):
        if not pair:
            return lax.psum_scatter(x, "shard", scatter_dimension=axis, tiled=True)
        size = x.shape[axis] // 2
        mine = lax.dynamic_slice_in_dim(x, c * size, size, axis=axis)
        theirs = lax.dynamic_slice_in_dim(x, (1 - c) * size, size, axis=axis)
        return mine + partner(theirs)

    def block_rows(grad_rows, k, c):
        start = k * cols
        if cols <= rows:
            piece = lax.dynamic_slice_in_dim(grad_rows, start % rows, cols, axis=0)
            owner = start // rows
            if pair:
                return jnp.where(owner == c, piece, partner(piece))
            pieces = lax.all_gather(piece, "shard", axis=0, tiled=False)
            return lax.dynamic_index_in_dim(pieces, owner, axis=0, keepdims=False)
        full = lax.all_gather(grad_rows, "shard", axis=0, tiled=True)
        return lax.dynamic_slice_in_dim(full, start, cols, axis=0)

    def all_sum(value):
        x = jnp.full((PAD, 128), value, jnp.float32)
        if n_ts & (n_ts - 1) == 0:
            step = 1
            while step < n_ts:
                x = x + lax.ppermute(x, TS, [(i, i ^ step) for i in range(n_ts)])
                step *= 2
        else:
            x = lax.psum(x, TS)
        return shard_sum(x)[0, 0]

    def newton_step(iterate):
        iterate_rows = lax.all_gather(iterate, TS, axis=1, tiled=True)
        z_cols = shard_sum(contract_rows(iterate_rows, iterate))
        return 1.5 * iterate - 0.5 * exact_dot(iterate_rows, z_cols)

    def shards(grad_parts, moment, second, stat_left, basis_left):
        c = lax.axis_index("shard")
        k = lax.axis_index("tensor") * n_section + lax.axis_index("section")
        part = grad_parts[0]
        if pair:
            mine = lax.dynamic_slice_in_dim(part, c * rows, rows, axis=1)
            theirs = lax.dynamic_slice_in_dim(part, (1 - c) * rows, rows, axis=1)
            grad_flip = (mine.astype(jnp.float32) + partner(theirs).astype(jnp.float32)).astype(jnp.bfloat16)
        else:
            grad_flip = lax.psum_scatter(
                part.astype(jnp.float32).astype(jnp.bfloat16), "shard", scatter_dimension=1, tiled=True
            )
        grad = grad_flip.T
        grad_cols = shard_concat(grad, c)
        basis_top = lax.reduce_precision(basis_left, exponent_bits=8, mantissa_bits=7)
        basis_hi = basis_top.astype(jnp.bfloat16)
        basis_lo = (basis_left - basis_top).astype(jnp.bfloat16)
        stacked = lax.all_gather(jnp.stack([grad, basis_hi, basis_lo]), TS, axis=2, tiled=True)
        grad_rows = stacked[0]
        basis_rows = stacked[1].astype(jnp.float32) + stacked[2].astype(jnp.float32)
        grad_krows = block_rows(grad_rows, k, c)
        gram = lax.dot_general(
            grad_rows, grad_krows, (((1,), (1,)), ((), ())), preferred_element_type=jnp.float32
        )
        stat_next = stat_decay * stat_left + (1.0 - stat_decay) / D * gram
        power = exact_dot(basis_rows, shard_concat(stat_next, c))
        power, basis_later = lax.optimization_barrier((power, basis_rows))
        rotated = exact_dot(basis_later, grad_cols.astype(jnp.float32))
        moment_next = beta_one * moment + (1.0 - beta_one) * rotated
        second_next = beta_two * second + (1.0 - beta_two) * rotated * rotated
        ratio = moment_next / first_fix / (jnp.sqrt(second_next / second_fix) + adam_eps)
        update = shard_sum_scatter(contract_rows(basis_later, ratio), c, 0)
        power_rows = lax.all_gather(power, TS, axis=1, tiled=True)
        total_sq = all_sum(jnp.sum(power * power))
        power_rows, update = lax.optimization_barrier((power_rows, update))
        z_cols = shard_sum(contract_rows(power_rows, power))
        scale = shrink * jnp.sqrt(D / (total_sq + norm_eps))
        iterate = (1.5 * scale) * power - (0.5 * scale * scale * scale) * exact_dot(power_rows, z_cols)
        for turn in range(NS_ITERS - 1):
            iterate = newton_step(iterate)
        return (update, moment_next, second_next, stat_next, iterate)

    return shards


def solution(mesh):
    n_shard = mesh.shape["shard"]
    n_section = mesh.shape["section"]
    n_ts = mesh.shape["tensor"] * n_section
    in_specs = (
        P("shard", TS, None),
        P("shard", TS),
        P("shard", TS),
        P("shard", TS),
        P("shard", TS),
    )
    out_specs = (
        P("shard", TS),
        P("shard", TS),
        P("shard", TS),
        P("shard", TS),
        P("shard", TS),
    )
    return jax.shard_map(
        make_shards(n_shard, n_section, n_ts), mesh=mesh, in_specs=in_specs, out_specs=out_specs, check_vma=False
    )
```

```python
import jax
import jax.numpy as jnp
from jax import lax
from jax.sharding import PartitionSpec as P

D = 2304
NS_ITERS = 2


beta_one = 0.9
beta_two = 0.95
stat_decay = 0.95
adam_eps = 1e-08
first_fix = 1.0 - 0.9**10
second_fix = 1.0 - 0.95**10
shrink = 0.6
norm_eps = 1e-06

TS = ("tensor", "section")
PAD = 8


def exact_dot(left, right):
    return jnp.dot(left, right, precision=lax.Precision.HIGH, preferred_element_type=jnp.float32)


def contract_rows(left, right):
    return lax.dot_general(
        left,
        right,
        (((0,), (0,)), ((), ())),
        precision=lax.Precision.HIGH,
        preferred_element_type=jnp.float32,
    )


def split_bf16(x):
    top = lax.reduce_precision(x, exponent_bits=8, mantissa_bits=7)
    return top.astype(jnp.bfloat16), (x - top).astype(jnp.bfloat16)


def bf16_dot(left, right, dims):
    return lax.dot_general(left, right, (dims, ((), ())), preferred_element_type=jnp.float32)


def split_dot(left_hi, left_lo, right, dims):
    right_hi, right_lo = split_bf16(right)
    return bf16_dot(left_hi, right_hi, dims) + bf16_dot(left_hi, right_lo, dims) + bf16_dot(left_lo, right_hi, dims)


def make_shards(n_shard, n_section, n_ts):
    rows = D // n_shard
    cols = D // n_ts
    assert rows % cols == 0 or cols % rows == 0
    pair = n_shard == 2

    def partner(x):
        return lax.ppermute(x, "shard", [(0, 1), (1, 0)])

    def shard_concat(x, c):
        if not pair:
            return lax.all_gather(x, "shard", axis=0, tiled=True)
        other = partner(x)
        first = jnp.where(c == 0, x, other)
        last = jnp.where(c == 0, other, x)
        return jnp.concatenate([first, last], axis=0)

    def shard_sum(x):
        if not pair:
            return lax.psum(x, "shard")
        return x + partner(x)

    def shard_sum_scatter(x, c, axis):
        if not pair:
            return lax.psum_scatter(x, "shard", scatter_dimension=axis, tiled=True)
        size = x.shape[axis] // 2
        mine = lax.dynamic_slice_in_dim(x, c * size, size, axis=axis)
        theirs = lax.dynamic_slice_in_dim(x, (1 - c) * size, size, axis=axis)
        return mine + partner(theirs)

    def block_rows(grad_rows, k, c):
        start = k * cols
        if cols <= rows:
            piece = lax.dynamic_slice_in_dim(grad_rows, start % rows, cols, axis=0)
            owner = start // rows
            if pair:
                return jnp.where(owner == c, piece, partner(piece))
            pieces = lax.all_gather(piece, "shard", axis=0, tiled=False)
            return lax.dynamic_index_in_dim(pieces, owner, axis=0, keepdims=False)
        full = lax.all_gather(grad_rows, "shard", axis=0, tiled=True)
        return lax.dynamic_slice_in_dim(full, start, cols, axis=0)

    def all_sum(value):
        x = jnp.full((PAD, 128), value, jnp.float32)
        if n_ts & (n_ts - 1) == 0:
            step = 1
            while step < n_ts:
                x = x + lax.ppermute(x, TS, [(i, i ^ step) for i in range(n_ts)])
                step *= 2
        else:
            x = lax.psum(x, TS)
        return shard_sum(x)[0, 0]

    def newton_step(iterate):
        iterate_rows = lax.all_gather(iterate, TS, axis=1, tiled=True)
        z_cols = shard_sum(contract_rows(iterate_rows, iterate))
        return 1.5 * iterate - 0.5 * exact_dot(iterate_rows, z_cols)

    def shards(grad_parts, moment, second, stat_left, basis_left):
        c = lax.axis_index("shard")
        k = lax.axis_index("tensor") * n_section + lax.axis_index("section")
        part = grad_parts[0]
        if pair:
            mine = lax.dynamic_slice_in_dim(part, c * rows, rows, axis=1)
            theirs = lax.dynamic_slice_in_dim(part, (1 - c) * rows, rows, axis=1)
            grad_flip = (mine.astype(jnp.float32) + partner(theirs).astype(jnp.float32)).astype(jnp.bfloat16)
        else:
            grad_flip = lax.psum_scatter(
                part.astype(jnp.float32).astype(jnp.bfloat16), "shard", scatter_dimension=1, tiled=True
            )
        grad = grad_flip.T
        grad_cols = shard_concat(grad, c)
        basis_hi, basis_lo = split_bf16(basis_left)
        stacked = lax.all_gather(jnp.stack([grad, basis_hi, basis_lo]), TS, axis=2, tiled=True)
        grad_rows, hi_rows, lo_rows = stacked[0], stacked[1], stacked[2]
        grad_krows = block_rows(grad_rows, k, c)
        gram = lax.dot_general(
            grad_rows, grad_krows, (((1,), (1,)), ((), ())), preferred_element_type=jnp.float32
        )
        stat_next = stat_decay * stat_left + (1.0 - stat_decay) / D * gram
        by_rows = ((1,), (0,))
        power = split_dot(hi_rows, lo_rows, shard_concat(stat_next, c), by_rows)
        power, hi_later, lo_later = lax.optimization_barrier((power, hi_rows, lo_rows))
        rotated = bf16_dot(hi_later, grad_cols, by_rows) + bf16_dot(lo_later, grad_cols, by_rows)
        moment_next = beta_one * moment + (1.0 - beta_one) * rotated
        second_next = beta_two * second + (1.0 - beta_two) * rotated * rotated
        ratio = moment_next / first_fix / (jnp.sqrt(second_next / second_fix) + adam_eps)
        update = shard_sum_scatter(split_dot(hi_later, lo_later, ratio, ((0,), (0,))), c, 0)
        power_rows = lax.all_gather(power, TS, axis=1, tiled=True)
        total_sq = all_sum(jnp.sum(power * power))
        power_rows, update, total_sq = lax.optimization_barrier((power_rows, update, total_sq))
        z_cols = shard_sum(contract_rows(power_rows, power))
        scale = shrink * jnp.sqrt(D / (total_sq + norm_eps))
        iterate = (1.5 * scale) * power - (0.5 * scale * scale * scale) * exact_dot(power_rows, z_cols)
        for turn in range(NS_ITERS - 1):
            iterate = newton_step(iterate)
        return (update, moment_next, second_next, stat_next, iterate)

    return shards


def solution(mesh):
    n_shard = mesh.shape["shard"]
    n_section = mesh.shape["section"]
    n_ts = mesh.shape["tensor"] * n_section
    in_specs = (
        P("shard", TS, None),
        P("shard", TS),
        P("shard", TS),
        P("shard", TS),
        P("shard", TS),
    )
    out_specs = (
        P("shard", TS),
        P("shard", TS),
        P("shard", TS),
        P("shard", TS),
        P("shard", TS),
    )
    return jax.shard_map(
        make_shards(n_shard, n_section, n_ts), mesh=mesh, in_specs=in_specs, out_specs=out_specs, check_vma=False
    )
```

```python
import jax
import jax.numpy as jnp
from jax import lax
from jax.sharding import PartitionSpec as P

D = 2304
NS_ITERS = 2


beta_one = 0.9
beta_two = 0.95
stat_decay = 0.95
adam_eps = 1e-08
first_fix = 1.0 - 0.9**10
second_fix = 1.0 - 0.95**10
shrink = 0.6
norm_eps = 1e-06

TS = ("tensor", "section")
PAD = 8


def exact_dot(left, right):
    return jnp.dot(left, right, precision=lax.Precision.HIGH, preferred_element_type=jnp.float32)


def contract_rows(left, right):
    return lax.dot_general(
        left,
        right,
        (((0,), (0,)), ((), ())),
        precision=lax.Precision.HIGH,
        preferred_element_type=jnp.float32,
    )


def split_bf16(x):
    top = lax.reduce_precision(x, exponent_bits=8, mantissa_bits=7)
    return top.astype(jnp.bfloat16), (x - top).astype(jnp.bfloat16)


def bf16_dot(left, right, dims):
    return lax.dot_general(left, right, (dims, ((), ())), preferred_element_type=jnp.float32)


def split_dot(left_hi, left_lo, right, dims):
    right_hi, right_lo = split_bf16(right)
    return bf16_dot(left_hi, right_hi, dims) + bf16_dot(left_hi, right_lo, dims) + bf16_dot(left_lo, right_hi, dims)


def make_shards(n_shard, n_section, n_ts):
    rows = D // n_shard
    cols = D // n_ts
    assert rows % cols == 0 or cols % rows == 0
    pair = n_shard == 2

    def partner(x):
        return lax.ppermute(x, "shard", [(0, 1), (1, 0)])

    def shard_concat(x, c):
        if not pair:
            return lax.all_gather(x, "shard", axis=0, tiled=True)
        other = partner(x)
        first = jnp.where(c == 0, x, other)
        last = jnp.where(c == 0, other, x)
        return jnp.concatenate([first, last], axis=0)

    def shard_sum(x):
        if not pair:
            return lax.psum(x, "shard")
        return x + partner(x)

    def shard_sum_scatter(x, c, axis):
        if not pair:
            return lax.psum_scatter(x, "shard", scatter_dimension=axis, tiled=True)
        size = x.shape[axis] // 2
        mine = lax.dynamic_slice_in_dim(x, c * size, size, axis=axis)
        theirs = lax.dynamic_slice_in_dim(x, (1 - c) * size, size, axis=axis)
        return mine + partner(theirs)

    def block_rows(grad_rows, k, c):
        start = k * cols
        if cols <= rows:
            piece = lax.dynamic_slice_in_dim(grad_rows, start % rows, cols, axis=0)
            owner = start // rows
            if pair:
                return jnp.where(owner == c, piece, partner(piece))
            pieces = lax.all_gather(piece, "shard", axis=0, tiled=False)
            return lax.dynamic_index_in_dim(pieces, owner, axis=0, keepdims=False)
        full = lax.all_gather(grad_rows, "shard", axis=0, tiled=True)
        return lax.dynamic_slice_in_dim(full, start, cols, axis=0)

    def all_sum(value):
        x = jnp.full((PAD, 128), value, jnp.float32)
        if n_ts & (n_ts - 1) == 0:
            step = 1
            while step < n_ts:
                x = x + lax.ppermute(x, TS, [(i, i ^ step) for i in range(n_ts)])
                step *= 2
        else:
            x = lax.psum(x, TS)
        return shard_sum(x)[0, 0]

    def newton_step(iterate):
        iterate_rows = lax.all_gather(iterate, TS, axis=1, tiled=True)
        z_cols = shard_sum(contract_rows(iterate_rows, iterate))
        return 1.5 * iterate - 0.5 * exact_dot(iterate_rows, z_cols)

    def shards(grad_parts, moment, second, stat_left, basis_left):
        c = lax.axis_index("shard")
        k = lax.axis_index("tensor") * n_section + lax.axis_index("section")
        part = grad_parts[0]
        if pair:
            mine = lax.dynamic_slice_in_dim(part, c * rows, rows, axis=1)
            theirs = lax.dynamic_slice_in_dim(part, (1 - c) * rows, rows, axis=1)
            grad_flip = (mine.astype(jnp.float32) + partner(theirs).astype(jnp.float32)).astype(jnp.bfloat16)
        else:
            grad_flip = lax.psum_scatter(
                part.astype(jnp.float32).astype(jnp.bfloat16), "shard", scatter_dimension=1, tiled=True
            )
        grad = grad_flip.T
        grad_cols = shard_concat(grad, c)
        basis_hi, basis_lo = split_bf16(basis_left)
        stacked = lax.all_gather(jnp.stack([grad, basis_hi, basis_lo]), TS, axis=2, tiled=True)
        grad_rows, hi_rows, lo_rows = stacked[0], stacked[1], stacked[2]
        grad_krows = block_rows(grad_rows, k, c)
        gram = lax.dot_general(
            grad_rows, grad_krows, (((1,), (1,)), ((), ())), preferred_element_type=jnp.float32
        )
        stat_next = stat_decay * stat_left + (1.0 - stat_decay) / D * gram
        by_rows = ((1,), (0,))
        power = split_dot(hi_rows, lo_rows, shard_concat(stat_next, c), by_rows)
        power, stacked_later = lax.optimization_barrier((power, stacked))
        hi_later, lo_later = stacked_later[1], stacked_later[2]
        rotated = bf16_dot(hi_later, grad_cols, by_rows) + bf16_dot(lo_later, grad_cols, by_rows)
        moment_next = beta_one * moment + (1.0 - beta_one) * rotated
        second_next = beta_two * second + (1.0 - beta_two) * rotated * rotated
        ratio = moment_next / first_fix / (jnp.sqrt(second_next / second_fix) + adam_eps)
        update = shard_sum_scatter(split_dot(hi_later, lo_later, ratio, ((0,), (0,))), c, 0)
        power_rows = lax.all_gather(power, TS, axis=1, tiled=True)
        total_sq = all_sum(jnp.sum(power * power))
        power_rows, update, total_sq = lax.optimization_barrier((power_rows, update, total_sq))
        z_cols = shard_sum(contract_rows(power_rows, power))
        scale = shrink * jnp.sqrt(D / (total_sq + norm_eps))
        iterate = (1.5 * scale) * power - (0.5 * scale * scale * scale) * exact_dot(power_rows, z_cols)
        for turn in range(NS_ITERS - 1):
            iterate = newton_step(iterate)
        return (update, moment_next, second_next, stat_next, iterate)

    return shards


def solution(mesh):
    n_shard = mesh.shape["shard"]
    n_section = mesh.shape["section"]
    n_ts = mesh.shape["tensor"] * n_section
    in_specs = (
        P("shard", TS, None),
        P("shard", TS),
        P("shard", TS),
        P("shard", TS),
        P("shard", TS),
    )
    out_specs = (
        P("shard", TS),
        P("shard", TS),
        P("shard", TS),
        P("shard", TS),
        P("shard", TS),
    )
    return jax.shard_map(
        make_shards(n_shard, n_section, n_ts), mesh=mesh, in_specs=in_specs, out_specs=out_specs, check_vma=False
    )
```

```python
import jax
import jax.numpy as jnp
from jax import lax
from jax.sharding import PartitionSpec as P

D = 2304
NS_ITERS = 2


beta_one = 0.9
beta_two = 0.95
stat_decay = 0.95
adam_eps = 1e-08
first_fix = 1.0 - 0.9**10
second_fix = 1.0 - 0.95**10
shrink = 0.6
norm_eps = 1e-06

TS = ("tensor", "section")
PAD = 8


def exact_dot(left, right):
    return jnp.dot(left, right, precision=lax.Precision.HIGH, preferred_element_type=jnp.float32)


def contract_rows(left, right):
    return lax.dot_general(
        left,
        right,
        (((0,), (0,)), ((), ())),
        precision=lax.Precision.HIGH,
        preferred_element_type=jnp.float32,
    )


def split_bf16(x):
    top = lax.reduce_precision(x, exponent_bits=8, mantissa_bits=7)
    return top.astype(jnp.bfloat16), (x - top).astype(jnp.bfloat16)


def bf16_dot(left, right, dims):
    return lax.dot_general(left, right, (dims, ((), ())), preferred_element_type=jnp.float32)


def split_dot(left_hi, left_lo, right, dims):
    right_hi, right_lo = split_bf16(right)
    return bf16_dot(left_hi, right_hi, dims) + bf16_dot(left_hi, right_lo, dims) + bf16_dot(left_lo, right_hi, dims)


def make_shards(n_shard, n_section, n_ts):
    rows = D // n_shard
    cols = D // n_ts
    assert rows % cols == 0 or cols % rows == 0
    pair = n_shard == 2

    def partner(x):
        return lax.ppermute(x, "shard", [(0, 1), (1, 0)])

    def shard_concat(x, c):
        if not pair:
            return lax.all_gather(x, "shard", axis=0, tiled=True)
        other = partner(x)
        first = jnp.where(c == 0, x, other)
        last = jnp.where(c == 0, other, x)
        return jnp.concatenate([first, last], axis=0)

    def shard_sum(x):
        if not pair:
            return lax.psum(x, "shard")
        return x + partner(x)

    def shard_sum_scatter(x, c, axis):
        if not pair:
            return lax.psum_scatter(x, "shard", scatter_dimension=axis, tiled=True)
        size = x.shape[axis] // 2
        mine = lax.dynamic_slice_in_dim(x, c * size, size, axis=axis)
        theirs = lax.dynamic_slice_in_dim(x, (1 - c) * size, size, axis=axis)
        return mine + partner(theirs)

    def block_rows(grad_rows, k, c):
        start = k * cols
        if cols <= rows:
            piece = lax.dynamic_slice_in_dim(grad_rows, start % rows, cols, axis=0)
            owner = start // rows
            if pair:
                return jnp.where(owner == c, piece, partner(piece))
            pieces = lax.all_gather(piece, "shard", axis=0, tiled=False)
            return lax.dynamic_index_in_dim(pieces, owner, axis=0, keepdims=False)
        full = lax.all_gather(grad_rows, "shard", axis=0, tiled=True)
        return lax.dynamic_slice_in_dim(full, start, cols, axis=0)

    def all_sum(value):
        x = jnp.full((PAD, 128), value, jnp.float32)
        if n_ts & (n_ts - 1) == 0:
            step = 1
            while step < n_ts:
                x = x + lax.ppermute(x, TS, [(i, i ^ step) for i in range(n_ts)])
                step *= 2
        else:
            x = lax.psum(x, TS)
        return shard_sum(x)[0, 0]

    def gather_split_rows(block):
        hi, lo = split_bf16(block)
        return lax.all_gather(jnp.stack([hi, lo]), TS, axis=2, tiled=True)

    def newton_products(split_rows, block):
        rows_hi, rows_lo = split_rows[0], split_rows[1]
        z_cols = shard_sum(split_dot(rows_hi, rows_lo, block, ((0,), (0,))))
        return split_dot(rows_hi, rows_lo, z_cols, ((1,), (0,)))

    def newton_step(iterate):
        return 1.5 * iterate - 0.5 * newton_products(gather_split_rows(iterate), iterate)

    def shards(grad_parts, moment, second, stat_left, basis_left):
        c = lax.axis_index("shard")
        k = lax.axis_index("tensor") * n_section + lax.axis_index("section")
        part = grad_parts[0]
        if pair:
            mine = lax.dynamic_slice_in_dim(part, c * rows, rows, axis=1)
            theirs = lax.dynamic_slice_in_dim(part, (1 - c) * rows, rows, axis=1)
            grad_flip = (mine.astype(jnp.float32) + partner(theirs).astype(jnp.float32)).astype(jnp.bfloat16)
        else:
            grad_flip = lax.psum_scatter(
                part.astype(jnp.float32).astype(jnp.bfloat16), "shard", scatter_dimension=1, tiled=True
            )
        grad = grad_flip.T
        grad_cols = shard_concat(grad, c)
        basis_hi, basis_lo = split_bf16(basis_left)
        stacked = lax.all_gather(jnp.stack([grad, basis_hi, basis_lo]), TS, axis=2, tiled=True)
        grad_rows, hi_rows, lo_rows = stacked[0], stacked[1], stacked[2]
        grad_krows = block_rows(grad_rows, k, c)
        gram = lax.dot_general(
            grad_rows, grad_krows, (((1,), (1,)), ((), ())), preferred_element_type=jnp.float32
        )
        stat_next = stat_decay * stat_left + (1.0 - stat_decay) / D * gram
        by_rows = ((1,), (0,))
        stat_hi, stat_lo = split_bf16(stat_next)
        stat_hi, stat_lo = shard_concat(stat_hi, c), shard_concat(stat_lo, c)
        power = (
            bf16_dot(hi_rows, stat_hi, by_rows) + bf16_dot(hi_rows, stat_lo, by_rows) + bf16_dot(lo_rows, stat_hi, by_rows)
        )
        power, stacked_later = lax.optimization_barrier((power, stacked))
        hi_later, lo_later = stacked_later[1], stacked_later[2]
        rotated = bf16_dot(hi_later, grad_cols, by_rows) + bf16_dot(lo_later, grad_cols, by_rows)
        moment_next = beta_one * moment + (1.0 - beta_one) * rotated
        second_next = beta_two * second + (1.0 - beta_two) * rotated * rotated
        ratio = moment_next / first_fix / (jnp.sqrt(second_next / second_fix) + adam_eps)
        update = shard_sum_scatter(split_dot(hi_later, lo_later, ratio, ((0,), (0,))), c, 0)
        power_rows = gather_split_rows(power)
        total_sq = all_sum(jnp.sum(power * power))
        power_rows, update, total_sq = lax.optimization_barrier((power_rows, update, total_sq))
        scale = shrink * jnp.sqrt(D / (total_sq + norm_eps))
        iterate = (1.5 * scale) * power - (0.5 * scale * scale * scale) * newton_products(power_rows, power)
        for turn in range(NS_ITERS - 1):
            iterate = newton_step(iterate)
        return (update, moment_next, second_next, stat_next, iterate)

    return shards


def solution(mesh):
    n_shard = mesh.shape["shard"]
    n_section = mesh.shape["section"]
    n_ts = mesh.shape["tensor"] * n_section
    in_specs = (
        P("shard", TS, None),
        P("shard", TS),
        P("shard", TS),
        P("shard", TS),
        P("shard", TS),
    )
    out_specs = (
        P("shard", TS),
        P("shard", TS),
        P("shard", TS),
        P("shard", TS),
        P("shard", TS),
    )
    return jax.shard_map(
        make_shards(n_shard, n_section, n_ts), mesh=mesh, in_specs=in_specs, out_specs=out_specs, check_vma=False
    )
```

```python
import jax
import jax.numpy as jnp
from jax import lax
from jax.sharding import PartitionSpec as P

D = 2304
NS_ITERS = 2


beta_one = 0.9
beta_two = 0.95
stat_decay = 0.95
adam_eps = 1e-08
first_fix = 1.0 - 0.9**10
second_fix = 1.0 - 0.95**10
shrink = 0.6
norm_eps = 1e-06

TS = ("tensor", "section")
PAD = 8


def exact_dot(left, right):
    return jnp.dot(left, right, precision=lax.Precision.HIGH, preferred_element_type=jnp.float32)


def contract_rows(left, right):
    return lax.dot_general(
        left,
        right,
        (((0,), (0,)), ((), ())),
        precision=lax.Precision.HIGH,
        preferred_element_type=jnp.float32,
    )


def split_bf16(x):
    top = lax.reduce_precision(x, exponent_bits=8, mantissa_bits=7)
    return top.astype(jnp.bfloat16), (x - top).astype(jnp.bfloat16)


def bf16_dot(left, right, dims):
    return lax.dot_general(left, right, (dims, ((), ())), preferred_element_type=jnp.float32)


def split_dot(left_hi, left_lo, right, dims):
    right_hi, right_lo = split_bf16(right)
    return bf16_dot(left_hi, right_hi, dims) + bf16_dot(left_hi, right_lo, dims) + bf16_dot(left_lo, right_hi, dims)


def make_shards(n_shard, n_section, n_ts):
    rows = D // n_shard
    cols = D // n_ts
    assert rows % cols == 0 or cols % rows == 0
    pair = n_shard == 2

    def partner(x):
        return lax.ppermute(x, "shard", [(0, 1), (1, 0)])

    def shard_concat(x, c):
        if not pair:
            return lax.all_gather(x, "shard", axis=0, tiled=True)
        other = partner(x)
        first = jnp.where(c == 0, x, other)
        last = jnp.where(c == 0, other, x)
        return jnp.concatenate([first, last], axis=0)

    def shard_sum(x):
        if not pair:
            return lax.psum(x, "shard")
        return x + partner(x)

    def shard_sum_scatter(x, c, axis):
        if not pair:
            return lax.psum_scatter(x, "shard", scatter_dimension=axis, tiled=True)
        size = x.shape[axis] // 2
        mine = lax.dynamic_slice_in_dim(x, c * size, size, axis=axis)
        theirs = lax.dynamic_slice_in_dim(x, (1 - c) * size, size, axis=axis)
        return mine + partner(theirs)

    def block_rows(grad_rows, k, c):
        start = k * cols
        if cols <= rows:
            piece = lax.dynamic_slice_in_dim(grad_rows, start % rows, cols, axis=0)
            owner = start // rows
            if pair:
                return jnp.where(owner == c, piece, partner(piece))
            pieces = lax.all_gather(piece, "shard", axis=0, tiled=False)
            return lax.dynamic_index_in_dim(pieces, owner, axis=0, keepdims=False)
        full = lax.all_gather(grad_rows, "shard", axis=0, tiled=True)
        return lax.dynamic_slice_in_dim(full, start, cols, axis=0)

    def all_sum(value):
        x = jnp.full((PAD, 128), value, jnp.float32)
        if n_ts & (n_ts - 1) == 0:
            step = 1
            while step < n_ts:
                x = x + lax.ppermute(x, TS, [(i, i ^ step) for i in range(n_ts)])
                step *= 2
        else:
            x = lax.psum(x, TS)
        return shard_sum(x)[0, 0]

    def newton_step(iterate):
        iterate_rows = lax.all_gather(iterate, TS, axis=1, tiled=True)
        z_cols = shard_sum(contract_rows(iterate_rows, iterate))
        return 1.5 * iterate - 0.5 * exact_dot(iterate_rows, z_cols)

    def shards(grad_parts, moment, second, stat_left, basis_left):
        c = lax.axis_index("shard")
        k = lax.axis_index("tensor") * n_section + lax.axis_index("section")
        part = grad_parts[0]
        if pair:
            mine = lax.dynamic_slice_in_dim(part, c * rows, rows, axis=1)
            theirs = lax.dynamic_slice_in_dim(part, (1 - c) * rows, rows, axis=1)
            grad_flip = (mine.astype(jnp.float32) + partner(theirs).astype(jnp.float32)).astype(jnp.bfloat16)
        else:
            grad_flip = lax.psum_scatter(
                part.astype(jnp.float32).astype(jnp.bfloat16), "shard", scatter_dimension=1, tiled=True
            )
        grad = grad_flip.T
        grad_cols = shard_concat(grad, c)
        basis_hi, basis_lo = split_bf16(basis_left)
        stacked = lax.all_gather(jnp.stack([grad, basis_hi, basis_lo]), TS, axis=2, tiled=True)
        grad_rows, hi_rows, lo_rows = stacked[0], stacked[1], stacked[2]
        grad_krows = block_rows(grad_rows, k, c)
        gram = lax.dot_general(
            grad_rows, grad_krows, (((1,), (1,)), ((), ())), preferred_element_type=jnp.float32
        )
        stat_next = stat_decay * stat_left + (1.0 - stat_decay) / D * gram
        by_rows = ((1,), (0,))
        stat_hi, stat_lo = split_bf16(shard_concat(stat_next, c))
        both = bf16_dot(hi_rows, jnp.concatenate([stat_hi, stat_lo], axis=1), by_rows)
        power = both[:, :cols] + both[:, cols:] + bf16_dot(lo_rows, stat_hi, by_rows)
        power, stacked_later = lax.optimization_barrier((power, stacked))
        hi_later, lo_later = stacked_later[1], stacked_later[2]
        rotated = bf16_dot(hi_later, grad_cols, by_rows) + bf16_dot(lo_later, grad_cols, by_rows)
        moment_next = beta_one * moment + (1.0 - beta_one) * rotated
        second_next = beta_two * second + (1.0 - beta_two) * rotated * rotated
        ratio = moment_next / first_fix / (jnp.sqrt(second_next / second_fix) + adam_eps)
        update = shard_sum_scatter(split_dot(hi_later, lo_later, ratio, ((0,), (0,))), c, 0)
        power_rows = lax.all_gather(power, TS, axis=1, tiled=True)
        total_sq = all_sum(jnp.sum(power * power))
        power_rows, update, total_sq = lax.optimization_barrier((power_rows, update, total_sq))
        z_cols = shard_sum(contract_rows(power_rows, power))
        scale = shrink * jnp.sqrt(D / (total_sq + norm_eps))
        iterate = (1.5 * scale) * power - (0.5 * scale * scale * scale) * exact_dot(power_rows, z_cols)
        for turn in range(NS_ITERS - 1):
            iterate = newton_step(iterate)
        return (update, moment_next, second_next, stat_next, iterate)

    return shards


def solution(mesh):
    n_shard = mesh.shape["shard"]
    n_section = mesh.shape["section"]
    n_ts = mesh.shape["tensor"] * n_section
    in_specs = (
        P("shard", TS, None),
        P("shard", TS),
        P("shard", TS),
        P("shard", TS),
        P("shard", TS),
    )
    out_specs = (
        P("shard", TS),
        P("shard", TS),
        P("shard", TS),
        P("shard", TS),
        P("shard", TS),
    )
    return jax.shard_map(
        make_shards(n_shard, n_section, n_ts), mesh=mesh, in_specs=in_specs, out_specs=out_specs, check_vma=False
    )
```

```python
import jax
import jax.numpy as jnp
from jax import lax
from jax.sharding import PartitionSpec as P

D = 2304
NS_ITERS = 2


beta_one = 0.9
beta_two = 0.95
stat_decay = 0.95
adam_eps = 1e-08
first_fix = 1.0 - 0.9**10
second_fix = 1.0 - 0.95**10
shrink = 0.6
norm_eps = 1e-06

TS = ("tensor", "section")
PAD = 8


def exact_dot(left, right):
    return jnp.dot(left, right, precision=lax.Precision.HIGH, preferred_element_type=jnp.float32)


def contract_rows(left, right):
    return lax.dot_general(
        left,
        right,
        (((0,), (0,)), ((), ())),
        precision=lax.Precision.HIGH,
        preferred_element_type=jnp.float32,
    )


def split_bf16(x):
    top = lax.reduce_precision(x, exponent_bits=8, mantissa_bits=7)
    return top.astype(jnp.bfloat16), (x - top).astype(jnp.bfloat16)


def bf16_dot(left, right, dims):
    return lax.dot_general(left, right, (dims, ((), ())), preferred_element_type=jnp.float32)


def split_dot(left_hi, left_lo, right, dims):
    right_hi, right_lo = split_bf16(right)
    return bf16_dot(left_hi, right_hi, dims) + bf16_dot(left_hi, right_lo, dims) + bf16_dot(left_lo, right_hi, dims)


def make_shards(n_shard, n_section, n_ts):
    rows = D // n_shard
    cols = D // n_ts
    assert rows % cols == 0 or cols % rows == 0
    pair = n_shard == 2

    def partner(x):
        return lax.ppermute(x, "shard", [(0, 1), (1, 0)])

    def shard_concat(x, c):
        if not pair:
            return lax.all_gather(x, "shard", axis=0, tiled=True)
        other = partner(x)
        first = jnp.where(c == 0, x, other)
        last = jnp.where(c == 0, other, x)
        return jnp.concatenate([first, last], axis=0)

    def shard_sum(x):
        if not pair:
            return lax.psum(x, "shard")
        return x + partner(x)

    def shard_sum_scatter(x, c, axis):
        if not pair:
            return lax.psum_scatter(x, "shard", scatter_dimension=axis, tiled=True)
        size = x.shape[axis] // 2
        mine = lax.dynamic_slice_in_dim(x, c * size, size, axis=axis)
        theirs = lax.dynamic_slice_in_dim(x, (1 - c) * size, size, axis=axis)
        return mine + partner(theirs)

    def block_rows(grad_rows, k, c):
        start = k * cols
        if cols <= rows:
            piece = lax.dynamic_slice_in_dim(grad_rows, start % rows, cols, axis=0)
            owner = start // rows
            if pair:
                return jnp.where(owner == c, piece, partner(piece))
            pieces = lax.all_gather(piece, "shard", axis=0, tiled=False)
            return lax.dynamic_index_in_dim(pieces, owner, axis=0, keepdims=False)
        full = lax.all_gather(grad_rows, "shard", axis=0, tiled=True)
        return lax.dynamic_slice_in_dim(full, start, cols, axis=0)

    def all_sum(value):
        x = jnp.full((PAD, 128), value, jnp.float32)
        if n_ts & (n_ts - 1) == 0:
            step = 1
            while step < n_ts:
                x = x + lax.ppermute(x, TS, [(i, i ^ step) for i in range(n_ts)])
                step *= 2
        else:
            x = lax.psum(x, TS)
        return shard_sum(x)[0, 0]

    def gather_split_rows(block):
        hi, lo = split_bf16(block)
        return lax.all_gather(jnp.stack([hi, lo]), TS, axis=2, tiled=True)

    def pair_dot(left_hi, left_lo, right, dims):
        right_hi, right_lo = split_bf16(right)
        width = right.shape[1]
        both = bf16_dot(left_hi, jnp.concatenate([right_hi, right_lo], axis=1), dims)
        return both[:, :width] + both[:, width:] + bf16_dot(left_lo, right_hi, dims)

    def newton_products(split_rows, block):
        rows_hi, rows_lo = split_rows[0], split_rows[1]
        z_cols = shard_sum(pair_dot(rows_hi, rows_lo, block, ((0,), (0,))))
        return pair_dot(rows_hi, rows_lo, z_cols, ((1,), (0,)))

    def newton_step(iterate):
        return 1.5 * iterate - 0.5 * newton_products(gather_split_rows(iterate), iterate)

    def shards(grad_parts, moment, second, stat_left, basis_left):
        c = lax.axis_index("shard")
        k = lax.axis_index("tensor") * n_section + lax.axis_index("section")
        part = grad_parts[0]
        if pair:
            mine = lax.dynamic_slice_in_dim(part, c * rows, rows, axis=1)
            theirs = lax.dynamic_slice_in_dim(part, (1 - c) * rows, rows, axis=1)
            grad_flip = (mine.astype(jnp.float32) + partner(theirs).astype(jnp.float32)).astype(jnp.bfloat16)
        else:
            grad_flip = lax.psum_scatter(
                part.astype(jnp.float32).astype(jnp.bfloat16), "shard", scatter_dimension=1, tiled=True
            )
        grad = grad_flip.T
        grad_cols = shard_concat(grad, c)
        basis_hi, basis_lo = split_bf16(basis_left)
        stacked = lax.all_gather(jnp.stack([grad, basis_hi, basis_lo]), TS, axis=2, tiled=True)
        grad_rows, hi_rows, lo_rows = stacked[0], stacked[1], stacked[2]
        grad_krows = block_rows(grad_rows, k, c)
        gram = lax.dot_general(
            grad_rows, grad_krows, (((1,), (1,)), ((), ())), preferred_element_type=jnp.float32
        )
        stat_next = stat_decay * stat_left + (1.0 - stat_decay) / D * gram
        by_rows = ((1,), (0,))
        stat_hi, stat_lo = split_bf16(shard_concat(stat_next, c))
        both = bf16_dot(hi_rows, jnp.concatenate([stat_hi, stat_lo], axis=1), by_rows)
        power = both[:, :cols] + both[:, cols:] + bf16_dot(lo_rows, stat_hi, by_rows)
        power, stacked_later = lax.optimization_barrier((power, stacked))
        hi_later, lo_later = stacked_later[1], stacked_later[2]
        rotated = bf16_dot(hi_later, grad_cols, by_rows) + bf16_dot(lo_later, grad_cols, by_rows)
        moment_next = beta_one * moment + (1.0 - beta_one) * rotated
        second_next = beta_two * second + (1.0 - beta_two) * rotated * rotated
        ratio = moment_next / first_fix / (jnp.sqrt(second_next / second_fix) + adam_eps)
        update = shard_sum_scatter(split_dot(hi_later, lo_later, ratio, ((0,), (0,))), c, 0)
        power_rows = gather_split_rows(power)
        total_sq = all_sum(jnp.sum(power * power))
        power_rows, update, total_sq = lax.optimization_barrier((power_rows, update, total_sq))
        scale = shrink * jnp.sqrt(D / (total_sq + norm_eps))
        iterate = (1.5 * scale) * power - (0.5 * scale * scale * scale) * newton_products(power_rows, power)
        for turn in range(NS_ITERS - 1):
            iterate = newton_step(iterate)
        return (update, moment_next, second_next, stat_next, iterate)

    return shards


def solution(mesh):
    n_shard = mesh.shape["shard"]
    n_section = mesh.shape["section"]
    n_ts = mesh.shape["tensor"] * n_section
    in_specs = (
        P("shard", TS, None),
        P("shard", TS),
        P("shard", TS),
        P("shard", TS),
        P("shard", TS),
    )
    out_specs = (
        P("shard", TS),
        P("shard", TS),
        P("shard", TS),
        P("shard", TS),
        P("shard", TS),
    )
    return jax.shard_map(
        make_shards(n_shard, n_section, n_ts), mesh=mesh, in_specs=in_specs, out_specs=out_specs, check_vma=False
    )
```

```python
import jax
import jax.numpy as jnp
from jax import lax
from jax.sharding import PartitionSpec as P

D = 2304
NS_ITERS = 2


beta_one = 0.9
beta_two = 0.95
stat_decay = 0.95
adam_eps = 1e-08
first_fix = 1.0 - 0.9**10
second_fix = 1.0 - 0.95**10
shrink = 0.6
norm_eps = 1e-06

TS = ("tensor", "section")
PAD = 8


def exact_dot(left, right):
    return jnp.dot(left, right, precision=lax.Precision.HIGH, preferred_element_type=jnp.float32)


def contract_rows(left, right):
    return lax.dot_general(
        left,
        right,
        (((0,), (0,)), ((), ())),
        precision=lax.Precision.HIGH,
        preferred_element_type=jnp.float32,
    )


def split_bf16(x):
    top = lax.reduce_precision(x, exponent_bits=8, mantissa_bits=7)
    return top.astype(jnp.bfloat16), (x - top).astype(jnp.bfloat16)


def bf16_dot(left, right, dims):
    return lax.dot_general(left, right, (dims, ((), ())), preferred_element_type=jnp.float32)


def split_dot(left_hi, left_lo, right, dims):
    right_hi, right_lo = split_bf16(right)
    return bf16_dot(left_hi, right_hi, dims) + bf16_dot(left_hi, right_lo, dims) + bf16_dot(left_lo, right_hi, dims)


def make_shards(n_shard, n_section, n_ts):
    rows = D // n_shard
    cols = D // n_ts
    assert rows % cols == 0 or cols % rows == 0
    pair = n_shard == 2

    def partner(x):
        return lax.ppermute(x, "shard", [(0, 1), (1, 0)])

    def shard_concat(x, c):
        if not pair:
            return lax.all_gather(x, "shard", axis=0, tiled=True)
        other = partner(x)
        first = jnp.where(c == 0, x, other)
        last = jnp.where(c == 0, other, x)
        return jnp.concatenate([first, last], axis=0)

    def shard_sum(x):
        if not pair:
            return lax.psum(x, "shard")
        return x + partner(x)

    def shard_sum_scatter(x, c, axis):
        if not pair:
            return lax.psum_scatter(x, "shard", scatter_dimension=axis, tiled=True)
        size = x.shape[axis] // 2
        mine = lax.dynamic_slice_in_dim(x, c * size, size, axis=axis)
        theirs = lax.dynamic_slice_in_dim(x, (1 - c) * size, size, axis=axis)
        return mine + partner(theirs)

    def block_rows(grad_rows, k, c):
        start = k * cols
        if cols <= rows:
            piece = lax.dynamic_slice_in_dim(grad_rows, start % rows, cols, axis=0)
            owner = start // rows
            if pair:
                return jnp.where(owner == c, piece, partner(piece))
            pieces = lax.all_gather(piece, "shard", axis=0, tiled=False)
            return lax.dynamic_index_in_dim(pieces, owner, axis=0, keepdims=False)
        full = lax.all_gather(grad_rows, "shard", axis=0, tiled=True)
        return lax.dynamic_slice_in_dim(full, start, cols, axis=0)

    def all_sum(value):
        x = jnp.full((PAD, 128), value, jnp.float32)
        if n_ts & (n_ts - 1) == 0:
            step = 1
            while step < n_ts:
                x = x + lax.ppermute(x, TS, [(i, i ^ step) for i in range(n_ts)])
                step *= 2
        else:
            x = lax.psum(x, TS)
        return shard_sum(x)[0, 0]

    def newton_step(iterate):
        iterate_rows = lax.all_gather(iterate, TS, axis=1, tiled=True)
        z_cols = shard_sum(contract_rows(iterate_rows, iterate))
        return 1.5 * iterate - 0.5 * exact_dot(iterate_rows, z_cols)

    def shards(grad_parts, moment, second, stat_left, basis_left):
        c = lax.axis_index("shard")
        k = lax.axis_index("tensor") * n_section + lax.axis_index("section")
        part = grad_parts[0]
        if pair:
            mine = lax.dynamic_slice_in_dim(part, c * rows, rows, axis=1)
            theirs = lax.dynamic_slice_in_dim(part, (1 - c) * rows, rows, axis=1)
            grad_flip = (mine.astype(jnp.float32) + partner(theirs).astype(jnp.float32)).astype(jnp.bfloat16)
        else:
            grad_flip = lax.psum_scatter(
                part.astype(jnp.float32).astype(jnp.bfloat16), "shard", scatter_dimension=1, tiled=True
            )
        grad = grad_flip.T
        grad_cols = shard_concat(grad, c)
        basis_hi, basis_lo = split_bf16(basis_left)
        stacked = lax.all_gather(jnp.stack([grad, basis_hi, basis_lo]), TS, axis=2, tiled=True)
        grad_rows, hi_rows, lo_rows = stacked[0], stacked[1], stacked[2]
        grad_krows = block_rows(grad_rows, k, c)
        gram = lax.dot_general(
            grad_rows, grad_krows, (((1,), (1,)), ((), ())), preferred_element_type=jnp.float32
        )
        stat_next = stat_decay * stat_left + (1.0 - stat_decay) / D * gram
        by_rows = ((1,), (0,))
        stat_hi, stat_lo = split_bf16(shard_concat(stat_next, c))
        quads = bf16_dot(stacked[1:], jnp.concatenate([stat_hi, stat_lo], axis=1), ((2,), (0,)))
        power = quads[0, :, :cols] + quads[0, :, cols:] + quads[1, :, :cols]
        power, stacked_later = lax.optimization_barrier((power, stacked))
        hi_later, lo_later = stacked_later[1], stacked_later[2]
        rotated = bf16_dot(hi_later, grad_cols, by_rows) + bf16_dot(lo_later, grad_cols, by_rows)
        moment_next = beta_one * moment + (1.0 - beta_one) * rotated
        second_next = beta_two * second + (1.0 - beta_two) * rotated * rotated
        ratio = moment_next / first_fix / (jnp.sqrt(second_next / second_fix) + adam_eps)
        update = shard_sum_scatter(split_dot(hi_later, lo_later, ratio, ((0,), (0,))), c, 0)
        power_rows = lax.all_gather(power, TS, axis=1, tiled=True)
        total_sq = all_sum(jnp.sum(power * power))
        power_rows, update, total_sq = lax.optimization_barrier((power_rows, update, total_sq))
        z_cols = shard_sum(contract_rows(power_rows, power))
        scale = shrink * jnp.sqrt(D / (total_sq + norm_eps))
        iterate = (1.5 * scale) * power - (0.5 * scale * scale * scale) * exact_dot(power_rows, z_cols)
        for turn in range(NS_ITERS - 1):
            iterate = newton_step(iterate)
        return (update, moment_next, second_next, stat_next, iterate)

    return shards


def solution(mesh):
    n_shard = mesh.shape["shard"]
    n_section = mesh.shape["section"]
    n_ts = mesh.shape["tensor"] * n_section
    in_specs = (
        P("shard", TS, None),
        P("shard", TS),
        P("shard", TS),
        P("shard", TS),
        P("shard", TS),
    )
    out_specs = (
        P("shard", TS),
        P("shard", TS),
        P("shard", TS),
        P("shard", TS),
        P("shard", TS),
    )
    return jax.shard_map(
        make_shards(n_shard, n_section, n_ts), mesh=mesh, in_specs=in_specs, out_specs=out_specs, check_vma=False
    )
```

```python
import jax
import jax.numpy as jnp
from jax import lax
from jax.sharding import PartitionSpec as P

D = 2304
NS_ITERS = 2


beta_one = 0.9
beta_two = 0.95
stat_decay = 0.95
adam_eps = 1e-08
first_fix = 1.0 - 0.9**10
second_fix = 1.0 - 0.95**10
shrink = 0.6
norm_eps = 1e-06

TS = ("tensor", "section")
PAD = 8


def exact_dot(left, right):
    return jnp.dot(left, right, precision=lax.Precision.HIGH, preferred_element_type=jnp.float32)


def contract_rows(left, right):
    return lax.dot_general(
        left,
        right,
        (((0,), (0,)), ((), ())),
        precision=lax.Precision.HIGH,
        preferred_element_type=jnp.float32,
    )


def split_bf16(x):
    top = lax.reduce_precision(x, exponent_bits=8, mantissa_bits=7)
    return top.astype(jnp.bfloat16), (x - top).astype(jnp.bfloat16)


def bf16_dot(left, right, dims):
    return lax.dot_general(left, right, (dims, ((), ())), preferred_element_type=jnp.float32)


def split_dot(left_hi, left_lo, right, dims):
    right_hi, right_lo = split_bf16(right)
    return bf16_dot(left_hi, right_hi, dims) + bf16_dot(left_hi, right_lo, dims) + bf16_dot(left_lo, right_hi, dims)


def make_shards(n_shard, n_section, n_ts):
    rows = D // n_shard
    cols = D // n_ts
    assert rows % cols == 0 or cols % rows == 0
    pair = n_shard == 2

    def partner(x):
        return lax.ppermute(x, "shard", [(0, 1), (1, 0)])

    def shard_concat(x, c):
        if not pair:
            return lax.all_gather(x, "shard", axis=0, tiled=True)
        other = partner(x)
        first = jnp.where(c == 0, x, other)
        last = jnp.where(c == 0, other, x)
        return jnp.concatenate([first, last], axis=0)

    def shard_sum(x):
        if not pair:
            return lax.psum(x, "shard")
        return x + partner(x)

    def shard_sum_scatter(x, c, axis):
        if not pair:
            return lax.psum_scatter(x, "shard", scatter_dimension=axis, tiled=True)
        size = x.shape[axis] // 2
        mine = lax.dynamic_slice_in_dim(x, c * size, size, axis=axis)
        theirs = lax.dynamic_slice_in_dim(x, (1 - c) * size, size, axis=axis)
        return mine + partner(theirs)

    def block_rows(grad_rows, k, c):
        start = k * cols
        if cols <= rows:
            piece = lax.dynamic_slice_in_dim(grad_rows, start % rows, cols, axis=0)
            owner = start // rows
            if pair:
                return jnp.where(owner == c, piece, partner(piece))
            pieces = lax.all_gather(piece, "shard", axis=0, tiled=False)
            return lax.dynamic_index_in_dim(pieces, owner, axis=0, keepdims=False)
        full = lax.all_gather(grad_rows, "shard", axis=0, tiled=True)
        return lax.dynamic_slice_in_dim(full, start, cols, axis=0)

    def all_sum(value):
        x = jnp.full((PAD, 128), value, jnp.float32)
        if n_ts & (n_ts - 1) == 0:
            step = 1
            while step < n_ts:
                x = x + lax.ppermute(x, TS, [(i, i ^ step) for i in range(n_ts)])
                step *= 2
        else:
            x = lax.psum(x, TS)
        return shard_sum(x)[0, 0]

    def gather_split_rows(block):
        hi, lo = split_bf16(block)
        return lax.all_gather(jnp.stack([hi, lo]), TS, axis=2, tiled=True)

    def quad_dot(split_left, right, axis):
        right_hi, right_lo = split_bf16(right)
        width = right.shape[1]
        quads = bf16_dot(split_left, jnp.concatenate([right_hi, right_lo], axis=1), ((axis,), (0,)))
        return quads[0, :, :width] + quads[0, :, width:] + quads[1, :, :width]

    def newton_products(split_rows, block):
        z_cols = shard_sum(quad_dot(split_rows, block, 1))
        return quad_dot(split_rows, z_cols, 2)

    def newton_step(iterate):
        return 1.5 * iterate - 0.5 * newton_products(gather_split_rows(iterate), iterate)

    def shards(grad_parts, moment, second, stat_left, basis_left):
        c = lax.axis_index("shard")
        k = lax.axis_index("tensor") * n_section + lax.axis_index("section")
        part = grad_parts[0]
        if pair:
            mine = lax.dynamic_slice_in_dim(part, c * rows, rows, axis=1)
            theirs = lax.dynamic_slice_in_dim(part, (1 - c) * rows, rows, axis=1)
            grad_flip = (mine.astype(jnp.float32) + partner(theirs).astype(jnp.float32)).astype(jnp.bfloat16)
        else:
            grad_flip = lax.psum_scatter(
                part.astype(jnp.float32).astype(jnp.bfloat16), "shard", scatter_dimension=1, tiled=True
            )
        grad = grad_flip.T
        grad_cols = shard_concat(grad, c)
        basis_hi, basis_lo = split_bf16(basis_left)
        stacked = lax.all_gather(jnp.stack([grad, basis_hi, basis_lo]), TS, axis=2, tiled=True)
        grad_rows, hi_rows, lo_rows = stacked[0], stacked[1], stacked[2]
        grad_krows = block_rows(grad_rows, k, c)
        gram = lax.dot_general(
            grad_rows, grad_krows, (((1,), (1,)), ((), ())), preferred_element_type=jnp.float32
        )
        stat_next = stat_decay * stat_left + (1.0 - stat_decay) / D * gram
        by_rows = ((1,), (0,))
        stat_hi, stat_lo = split_bf16(shard_concat(stat_next, c))
        quads = bf16_dot(stacked[1:], jnp.concatenate([stat_hi, stat_lo], axis=1), ((2,), (0,)))
        power = quads[0, :, :cols] + quads[0, :, cols:] + quads[1, :, :cols]
        power, stacked_later = lax.optimization_barrier((power, stacked))
        hi_later, lo_later = stacked_later[1], stacked_later[2]
        rotated = bf16_dot(hi_later, grad_cols, by_rows) + bf16_dot(lo_later, grad_cols, by_rows)
        moment_next = beta_one * moment + (1.0 - beta_one) * rotated
        second_next = beta_two * second + (1.0 - beta_two) * rotated * rotated
        ratio = moment_next / first_fix / (jnp.sqrt(second_next / second_fix) + adam_eps)
        update = shard_sum_scatter(split_dot(hi_later, lo_later, ratio, ((0,), (0,))), c, 0)
        power_rows = gather_split_rows(power)
        total_sq = all_sum(jnp.sum(power * power))
        power_rows, update, total_sq = lax.optimization_barrier((power_rows, update, total_sq))
        scale = shrink * jnp.sqrt(D / (total_sq + norm_eps))
        iterate = (1.5 * scale) * power - (0.5 * scale * scale * scale) * newton_products(power_rows, power)
        for turn in range(NS_ITERS - 1):
            iterate = newton_step(iterate)
        return (update, moment_next, second_next, stat_next, iterate)

    return shards


def solution(mesh):
    n_shard = mesh.shape["shard"]
    n_section = mesh.shape["section"]
    n_ts = mesh.shape["tensor"] * n_section
    in_specs = (
        P("shard", TS, None),
        P("shard", TS),
        P("shard", TS),
        P("shard", TS),
        P("shard", TS),
    )
    out_specs = (
        P("shard", TS),
        P("shard", TS),
        P("shard", TS),
        P("shard", TS),
        P("shard", TS),
    )
    return jax.shard_map(
        make_shards(n_shard, n_section, n_ts), mesh=mesh, in_specs=in_specs, out_specs=out_specs, check_vma=False
    )
```

```python
import jax
import jax.numpy as jnp
from jax import lax
from jax.sharding import PartitionSpec as P

D = 2304
NS_ITERS = 2


beta_one = 0.9
beta_two = 0.95
stat_decay = 0.95
adam_eps = 1e-08
first_fix = 1.0 - 0.9**10
second_fix = 1.0 - 0.95**10
shrink = 0.6
norm_eps = 1e-06

TS = ("tensor", "section")
PAD = 8


def exact_dot(left, right):
    return jnp.dot(left, right, precision=lax.Precision.HIGH, preferred_element_type=jnp.float32)


def contract_rows(left, right):
    return lax.dot_general(
        left,
        right,
        (((0,), (0,)), ((), ())),
        precision=lax.Precision.HIGH,
        preferred_element_type=jnp.float32,
    )


def split_bf16(x):
    top = lax.reduce_precision(x, exponent_bits=8, mantissa_bits=7)
    return top.astype(jnp.bfloat16), (x - top).astype(jnp.bfloat16)


def bf16_dot(left, right, dims):
    return lax.dot_general(left, right, (dims, ((), ())), preferred_element_type=jnp.float32)


def split_dot(left_hi, left_lo, right, dims):
    right_hi, right_lo = split_bf16(right)
    return bf16_dot(left_hi, right_hi, dims) + bf16_dot(left_hi, right_lo, dims) + bf16_dot(left_lo, right_hi, dims)


def make_shards(n_shard, n_section, n_ts):
    rows = D // n_shard
    cols = D // n_ts
    assert rows % cols == 0 or cols % rows == 0
    pair = n_shard == 2

    def partner(x):
        return lax.ppermute(x, "shard", [(0, 1), (1, 0)])

    def shard_concat(x, c):
        if not pair:
            return lax.all_gather(x, "shard", axis=0, tiled=True)
        other = partner(x)
        first = jnp.where(c == 0, x, other)
        last = jnp.where(c == 0, other, x)
        return jnp.concatenate([first, last], axis=0)

    def shard_sum(x):
        if not pair:
            return lax.psum(x, "shard")
        return x + partner(x)

    def shard_sum_scatter(x, c, axis):
        if not pair:
            return lax.psum_scatter(x, "shard", scatter_dimension=axis, tiled=True)
        size = x.shape[axis] // 2
        mine = lax.dynamic_slice_in_dim(x, c * size, size, axis=axis)
        theirs = lax.dynamic_slice_in_dim(x, (1 - c) * size, size, axis=axis)
        return mine + partner(theirs)

    def block_rows(grad_rows, k, c):
        start = k * cols
        if cols <= rows:
            piece = lax.dynamic_slice_in_dim(grad_rows, start % rows, cols, axis=0)
            owner = start // rows
            if pair:
                return jnp.where(owner == c, piece, partner(piece))
            pieces = lax.all_gather(piece, "shard", axis=0, tiled=False)
            return lax.dynamic_index_in_dim(pieces, owner, axis=0, keepdims=False)
        full = lax.all_gather(grad_rows, "shard", axis=0, tiled=True)
        return lax.dynamic_slice_in_dim(full, start, cols, axis=0)

    def all_sum(value):
        x = jnp.full((PAD, 128), value, jnp.float32)
        if n_ts & (n_ts - 1) == 0:
            step = 1
            while step < n_ts:
                x = x + lax.ppermute(x, TS, [(i, i ^ step) for i in range(n_ts)])
                step *= 2
        else:
            x = lax.psum(x, TS)
        return shard_sum(x)[0, 0]

    def newton_step(iterate):
        iterate_rows = lax.all_gather(iterate, TS, axis=1, tiled=True)
        z_cols = shard_sum(contract_rows(iterate_rows, iterate))
        return 1.5 * iterate - 0.5 * exact_dot(iterate_rows, z_cols)

    def shards(grad_parts, moment, second, stat_left, basis_left):
        c = lax.axis_index("shard")
        k = lax.axis_index("tensor") * n_section + lax.axis_index("section")
        part = grad_parts[0]
        if pair:
            mine = lax.dynamic_slice_in_dim(part, c * rows, rows, axis=1)
            theirs = lax.dynamic_slice_in_dim(part, (1 - c) * rows, rows, axis=1)
            grad_flip = (mine.astype(jnp.float32) + partner(theirs).astype(jnp.float32)).astype(jnp.bfloat16)
        else:
            grad_flip = lax.psum_scatter(
                part.astype(jnp.float32).astype(jnp.bfloat16), "shard", scatter_dimension=1, tiled=True
            )
        grad = grad_flip.T
        grad_cols = shard_concat(grad, c)
        basis_hi, basis_lo = split_bf16(basis_left)
        stacked = lax.all_gather(jnp.stack([grad, basis_hi, basis_lo]), TS, axis=2, tiled=True)
        grad_rows, hi_rows, lo_rows = stacked[0], stacked[1], stacked[2]
        if cols <= rows and pair:
            piece = lax.dynamic_slice(stacked, (0, (k * cols) % rows, 0), (1, cols, D))[0]
            grad_krows = jnp.where((k * cols) // rows == c, piece, partner(piece))
        else:
            grad_krows = block_rows(grad_rows, k, c)
        gram = lax.dot_general(
            grad_rows, grad_krows, (((1,), (1,)), ((), ())), preferred_element_type=jnp.float32
        )
        stat_next = stat_decay * stat_left + (1.0 - stat_decay) / D * gram
        by_rows = ((1,), (0,))
        stat_hi, stat_lo = split_bf16(shard_concat(stat_next, c))
        quads = bf16_dot(stacked[1:], jnp.concatenate([stat_hi, stat_lo], axis=1), ((2,), (0,)))
        power = quads[0, :, :cols] + quads[0, :, cols:] + quads[1, :, :cols]
        power, stacked_later = lax.optimization_barrier((power, stacked))
        hi_later, lo_later = stacked_later[1], stacked_later[2]
        rotated = bf16_dot(hi_later, grad_cols, by_rows) + bf16_dot(lo_later, grad_cols, by_rows)
        moment_next = beta_one * moment + (1.0 - beta_one) * rotated
        second_next = beta_two * second + (1.0 - beta_two) * rotated * rotated
        ratio = moment_next / first_fix / (jnp.sqrt(second_next / second_fix) + adam_eps)
        update = shard_sum_scatter(split_dot(hi_later, lo_later, ratio, ((0,), (0,))), c, 0)
        power_rows = lax.all_gather(power, TS, axis=1, tiled=True)
        total_sq = all_sum(jnp.sum(power * power))
        power_rows, update, total_sq = lax.optimization_barrier((power_rows, update, total_sq))
        z_cols = shard_sum(contract_rows(power_rows, power))
        scale = shrink * jnp.sqrt(D / (total_sq + norm_eps))
        iterate = (1.5 * scale) * power - (0.5 * scale * scale * scale) * exact_dot(power_rows, z_cols)
        for turn in range(NS_ITERS - 1):
            iterate = newton_step(iterate)
        return (update, moment_next, second_next, stat_next, iterate)

    return shards


def solution(mesh):
    n_shard = mesh.shape["shard"]
    n_section = mesh.shape["section"]
    n_ts = mesh.shape["tensor"] * n_section
    in_specs = (
        P("shard", TS, None),
        P("shard", TS),
        P("shard", TS),
        P("shard", TS),
        P("shard", TS),
    )
    out_specs = (
        P("shard", TS),
        P("shard", TS),
        P("shard", TS),
        P("shard", TS),
        P("shard", TS),
    )
    return jax.shard_map(
        make_shards(n_shard, n_section, n_ts), mesh=mesh, in_specs=in_specs, out_specs=out_specs, check_vma=False
    )
```

```python
import jax
import jax.numpy as jnp
from jax import lax
from jax.sharding import PartitionSpec as P

D = 2304
NS_ITERS = 2


beta_one = 0.9
beta_two = 0.95
stat_decay = 0.95
adam_eps = 1e-08
first_fix = 1.0 - 0.9**10
second_fix = 1.0 - 0.95**10
shrink = 0.6
norm_eps = 1e-06

TS = ("tensor", "section")
PAD = 8


def exact_dot(left, right):
    return jnp.dot(left, right, precision=lax.Precision.HIGH, preferred_element_type=jnp.float32)


def contract_rows(left, right):
    return lax.dot_general(
        left,
        right,
        (((0,), (0,)), ((), ())),
        precision=lax.Precision.HIGH,
        preferred_element_type=jnp.float32,
    )


def split_bf16(x):
    top = lax.reduce_precision(x, exponent_bits=8, mantissa_bits=7)
    return top.astype(jnp.bfloat16), (x - top).astype(jnp.bfloat16)


def bf16_dot(left, right, dims):
    return lax.dot_general(left, right, (dims, ((), ())), preferred_element_type=jnp.float32)


def split_dot(left_hi, left_lo, right, dims):
    right_hi, right_lo = split_bf16(right)
    return bf16_dot(left_hi, right_hi, dims) + bf16_dot(left_hi, right_lo, dims) + bf16_dot(left_lo, right_hi, dims)


def make_shards(n_shard, n_section, n_ts):
    rows = D // n_shard
    cols = D // n_ts
    assert rows % cols == 0 or cols % rows == 0
    pair = n_shard == 2

    def partner(x):
        return lax.ppermute(x, "shard", [(0, 1), (1, 0)])

    def shard_concat(x, c):
        if not pair:
            return lax.all_gather(x, "shard", axis=0, tiled=True)
        other = partner(x)
        first = jnp.where(c == 0, x, other)
        last = jnp.where(c == 0, other, x)
        return jnp.concatenate([first, last], axis=0)

    def shard_sum(x):
        if not pair:
            return lax.psum(x, "shard")
        return x + partner(x)

    def shard_sum_scatter(x, c, axis):
        if not pair:
            return lax.psum_scatter(x, "shard", scatter_dimension=axis, tiled=True)
        size = x.shape[axis] // 2
        mine = lax.dynamic_slice_in_dim(x, c * size, size, axis=axis)
        theirs = lax.dynamic_slice_in_dim(x, (1 - c) * size, size, axis=axis)
        return mine + partner(theirs)

    def block_rows(grad_rows, k, c):
        start = k * cols
        if cols <= rows:
            piece = lax.dynamic_slice_in_dim(grad_rows, start % rows, cols, axis=0)
            owner = start // rows
            if pair:
                return jnp.where(owner == c, piece, partner(piece))
            pieces = lax.all_gather(piece, "shard", axis=0, tiled=False)
            return lax.dynamic_index_in_dim(pieces, owner, axis=0, keepdims=False)
        full = lax.all_gather(grad_rows, "shard", axis=0, tiled=True)
        return lax.dynamic_slice_in_dim(full, start, cols, axis=0)

    def all_sum(value):
        x = jnp.full((PAD, 128), value, jnp.float32)
        if n_ts & (n_ts - 1) == 0:
            step = 1
            while step < n_ts:
                x = x + lax.ppermute(x, TS, [(i, i ^ step) for i in range(n_ts)])
                step *= 2
        else:
            x = lax.psum(x, TS)
        return shard_sum(x)[0, 0]

    def newton_step(iterate):
        iterate_rows = lax.all_gather(iterate, TS, axis=1, tiled=True)
        z_cols = shard_sum(contract_rows(iterate_rows, iterate))
        return 1.5 * iterate - 0.5 * exact_dot(iterate_rows, z_cols)

    def shards(grad_parts, moment, second, stat_left, basis_left):
        c = lax.axis_index("shard")
        k = lax.axis_index("tensor") * n_section + lax.axis_index("section")
        part = grad_parts[0]
        if pair:
            mine = lax.dynamic_slice_in_dim(part, c * rows, rows, axis=1)
            theirs = lax.dynamic_slice_in_dim(part, (1 - c) * rows, rows, axis=1)
            grad_flip = (mine.astype(jnp.float32) + partner(theirs).astype(jnp.float32)).astype(jnp.bfloat16)
        else:
            grad_flip = lax.psum_scatter(
                part.astype(jnp.float32).astype(jnp.bfloat16), "shard", scatter_dimension=1, tiled=True
            )
        grad = grad_flip.T
        grad_cols = shard_concat(grad, c)
        basis_hi, basis_lo = split_bf16(basis_left)
        stacked = lax.all_gather(jnp.stack([grad, basis_hi, basis_lo]), TS, axis=2, tiled=True)
        grad_rows, hi_rows, lo_rows = stacked[0], stacked[1], stacked[2]
        if cols <= rows and pair:
            piece = lax.dynamic_slice(stacked, (0, (k * cols) % rows, 0), (1, cols, D))[0]
            grad_krows = jnp.where((k * cols) // rows == c, piece, partner(piece))
        else:
            grad_krows = block_rows(grad_rows, k, c)
        gram = lax.dot_general(
            grad_rows, grad_krows, (((1,), (1,)), ((), ())), preferred_element_type=jnp.float32
        )
        stat_next = stat_decay * stat_left + (1.0 - stat_decay) / D * gram
        by_rows = ((1,), (0,))
        stat_hi, stat_lo = split_bf16(stat_next)
        stat_hi, stat_lo = shard_concat(stat_hi, c), shard_concat(stat_lo, c)
        quads = bf16_dot(stacked[1:], jnp.concatenate([stat_hi, stat_lo], axis=1), ((2,), (0,)))
        power = quads[0, :, :cols] + quads[0, :, cols:] + quads[1, :, :cols]
        power, stacked_later = lax.optimization_barrier((power, stacked))
        hi_later, lo_later = stacked_later[1], stacked_later[2]
        rotated = bf16_dot(hi_later, grad_cols, by_rows) + bf16_dot(lo_later, grad_cols, by_rows)
        moment_next = beta_one * moment + (1.0 - beta_one) * rotated
        second_next = beta_two * second + (1.0 - beta_two) * rotated * rotated
        ratio = moment_next / first_fix / (jnp.sqrt(second_next / second_fix) + adam_eps)
        update = shard_sum_scatter(split_dot(hi_later, lo_later, ratio, ((0,), (0,))), c, 0)
        power_rows = lax.all_gather(power, TS, axis=1, tiled=True)
        total_sq = all_sum(jnp.sum(power * power))
        power_rows, update, total_sq = lax.optimization_barrier((power_rows, update, total_sq))
        z_cols = shard_sum(contract_rows(power_rows, power))
        scale = shrink * jnp.sqrt(D / (total_sq + norm_eps))
        iterate = (1.5 * scale) * power - (0.5 * scale * scale * scale) * exact_dot(power_rows, z_cols)
        for turn in range(NS_ITERS - 1):
            iterate = newton_step(iterate)
        return (update, moment_next, second_next, stat_next, iterate)

    return shards


def solution(mesh):
    n_shard = mesh.shape["shard"]
    n_section = mesh.shape["section"]
    n_ts = mesh.shape["tensor"] * n_section
    in_specs = (
        P("shard", TS, None),
        P("shard", TS),
        P("shard", TS),
        P("shard", TS),
        P("shard", TS),
    )
    out_specs = (
        P("shard", TS),
        P("shard", TS),
        P("shard", TS),
        P("shard", TS),
        P("shard", TS),
    )
    return jax.shard_map(
        make_shards(n_shard, n_section, n_ts), mesh=mesh, in_specs=in_specs, out_specs=out_specs, check_vma=False
    )
```

```python
import jax
import jax.numpy as jnp
from jax import lax
from jax.sharding import PartitionSpec as P

D = 2304
NS_ITERS = 2


beta_one = 0.9
beta_two = 0.95
stat_decay = 0.95
adam_eps = 1e-08
first_fix = 1.0 - 0.9**10
second_fix = 1.0 - 0.95**10
shrink = 0.6
norm_eps = 1e-06

TS = ("tensor", "section")
PAD = 8


def exact_dot(left, right):
    return jnp.dot(left, right, precision=lax.Precision.HIGH, preferred_element_type=jnp.float32)


def contract_rows(left, right):
    return lax.dot_general(
        left,
        right,
        (((0,), (0,)), ((), ())),
        precision=lax.Precision.HIGH,
        preferred_element_type=jnp.float32,
    )


def split_bf16(x):
    top = lax.reduce_precision(x, exponent_bits=8, mantissa_bits=7)
    return top.astype(jnp.bfloat16), (x - top).astype(jnp.bfloat16)


def bf16_dot(left, right, dims):
    return lax.dot_general(left, right, (dims, ((), ())), preferred_element_type=jnp.float32)


def split_dot(left_hi, left_lo, right, dims):
    right_hi, right_lo = split_bf16(right)
    return bf16_dot(left_hi, right_hi, dims) + bf16_dot(left_hi, right_lo, dims) + bf16_dot(left_lo, right_hi, dims)


def make_shards(n_shard, n_section, n_ts):
    rows = D // n_shard
    cols = D // n_ts
    assert rows % cols == 0 or cols % rows == 0
    pair = n_shard == 2

    def partner(x):
        return lax.ppermute(x, "shard", [(0, 1), (1, 0)])

    def shard_concat(x, c):
        if not pair:
            return lax.all_gather(x, "shard", axis=0, tiled=True)
        other = partner(x)
        first = jnp.where(c == 0, x, other)
        last = jnp.where(c == 0, other, x)
        return jnp.concatenate([first, last], axis=0)

    def shard_sum(x):
        if not pair:
            return lax.psum(x, "shard")
        return x + partner(x)

    def shard_sum_scatter(x, c, axis):
        if not pair:
            return lax.psum_scatter(x, "shard", scatter_dimension=axis, tiled=True)
        size = x.shape[axis] // 2
        mine = lax.dynamic_slice_in_dim(x, c * size, size, axis=axis)
        theirs = lax.dynamic_slice_in_dim(x, (1 - c) * size, size, axis=axis)
        return mine + partner(theirs)

    def block_rows(grad_rows, k, c):
        start = k * cols
        if cols <= rows:
            piece = lax.dynamic_slice_in_dim(grad_rows, start % rows, cols, axis=0)
            owner = start // rows
            if pair:
                return jnp.where(owner == c, piece, partner(piece))
            pieces = lax.all_gather(piece, "shard", axis=0, tiled=False)
            return lax.dynamic_index_in_dim(pieces, owner, axis=0, keepdims=False)
        full = lax.all_gather(grad_rows, "shard", axis=0, tiled=True)
        return lax.dynamic_slice_in_dim(full, start, cols, axis=0)

    def all_sum(value):
        x = jnp.full((PAD, 128), value, jnp.float32)
        if n_ts & (n_ts - 1) == 0:
            step = 1
            while step < n_ts:
                x = x + lax.ppermute(x, TS, [(i, i ^ step) for i in range(n_ts)])
                step *= 2
        else:
            x = lax.psum(x, TS)
        return shard_sum(x)[0, 0]

    def newton_products(rows_all, block):
        half = cols // 2
        parts = []
        for lo_col in (0, half):
            z_half = shard_sum(contract_rows(rows_all, block[:, lo_col:lo_col + half]))
            parts.append(exact_dot(rows_all, z_half))
        return jnp.concatenate(parts, axis=1)

    def newton_step(iterate):
        iterate_rows = lax.all_gather(iterate, TS, axis=1, tiled=True)
        return 1.5 * iterate - 0.5 * newton_products(iterate_rows, iterate)

    def shards(grad_parts, moment, second, stat_left, basis_left):
        c = lax.axis_index("shard")
        k = lax.axis_index("tensor") * n_section + lax.axis_index("section")
        part = grad_parts[0]
        if pair:
            mine = lax.dynamic_slice_in_dim(part, c * rows, rows, axis=1)
            theirs = lax.dynamic_slice_in_dim(part, (1 - c) * rows, rows, axis=1)
            grad_flip = (mine.astype(jnp.float32) + partner(theirs).astype(jnp.float32)).astype(jnp.bfloat16)
        else:
            grad_flip = lax.psum_scatter(
                part.astype(jnp.float32).astype(jnp.bfloat16), "shard", scatter_dimension=1, tiled=True
            )
        grad = grad_flip.T
        grad_cols = shard_concat(grad, c)
        basis_hi, basis_lo = split_bf16(basis_left)
        stacked = lax.all_gather(jnp.stack([grad, basis_hi, basis_lo]), TS, axis=2, tiled=True)
        grad_rows, hi_rows, lo_rows = stacked[0], stacked[1], stacked[2]
        if cols <= rows and pair:
            piece = lax.dynamic_slice(stacked, (0, (k * cols) % rows, 0), (1, cols, D))[0]
            grad_krows = jnp.where((k * cols) // rows == c, piece, partner(piece))
        else:
            grad_krows = block_rows(grad_rows, k, c)
        gram = lax.dot_general(
            grad_rows, grad_krows, (((1,), (1,)), ((), ())), preferred_element_type=jnp.float32
        )
        stat_next = stat_decay * stat_left + (1.0 - stat_decay) / D * gram
        by_rows = ((1,), (0,))
        stat_hi, stat_lo = split_bf16(shard_concat(stat_next, c))
        quads = bf16_dot(stacked[1:], jnp.concatenate([stat_hi, stat_lo], axis=1), ((2,), (0,)))
        power = quads[0, :, :cols] + quads[0, :, cols:] + quads[1, :, :cols]
        power, stacked_later = lax.optimization_barrier((power, stacked))
        hi_later, lo_later = stacked_later[1], stacked_later[2]
        rotated = bf16_dot(hi_later, grad_cols, by_rows) + bf16_dot(lo_later, grad_cols, by_rows)
        moment_next = beta_one * moment + (1.0 - beta_one) * rotated
        second_next = beta_two * second + (1.0 - beta_two) * rotated * rotated
        ratio = moment_next / first_fix / (jnp.sqrt(second_next / second_fix) + adam_eps)
        update = shard_sum_scatter(split_dot(hi_later, lo_later, ratio, ((0,), (0,))), c, 0)
        power_rows = lax.all_gather(power, TS, axis=1, tiled=True)
        total_sq = all_sum(jnp.sum(power * power))
        power_rows, update, total_sq = lax.optimization_barrier((power_rows, update, total_sq))
        scale = shrink * jnp.sqrt(D / (total_sq + norm_eps))
        iterate = (1.5 * scale) * power - (0.5 * scale * scale * scale) * newton_products(power_rows, power)
        for turn in range(NS_ITERS - 1):
            iterate = newton_step(iterate)
        return (update, moment_next, second_next, stat_next, iterate)

    return shards


def solution(mesh):
    n_shard = mesh.shape["shard"]
    n_section = mesh.shape["section"]
    n_ts = mesh.shape["tensor"] * n_section
    in_specs = (
        P("shard", TS, None),
        P("shard", TS),
        P("shard", TS),
        P("shard", TS),
        P("shard", TS),
    )
    out_specs = (
        P("shard", TS),
        P("shard", TS),
        P("shard", TS),
        P("shard", TS),
        P("shard", TS),
    )
    return jax.shard_map(
        make_shards(n_shard, n_section, n_ts), mesh=mesh, in_specs=in_specs, out_specs=out_specs, check_vma=False
    )
```

```python
import jax
import jax.numpy as jnp
from jax import lax
from jax.sharding import PartitionSpec as P

D = 2304
NS_ITERS = 2


beta_one = 0.9
beta_two = 0.95
stat_decay = 0.95
adam_eps = 1e-08
first_fix = 1.0 - 0.9**10
second_fix = 1.0 - 0.95**10
shrink = 0.6
norm_eps = 1e-06

TS = ("tensor", "section")
PAD = 8


def exact_dot(left, right):
    return jnp.dot(left, right, precision=lax.Precision.HIGH, preferred_element_type=jnp.float32)


def contract_rows(left, right):
    return lax.dot_general(
        left,
        right,
        (((0,), (0,)), ((), ())),
        precision=lax.Precision.HIGH,
        preferred_element_type=jnp.float32,
    )


def split_bf16(x):
    top = lax.reduce_precision(x, exponent_bits=8, mantissa_bits=7)
    return top.astype(jnp.bfloat16), (x - top).astype(jnp.bfloat16)


def bf16_dot(left, right, dims):
    return lax.dot_general(left, right, (dims, ((), ())), preferred_element_type=jnp.float32)


def split_dot(left_hi, left_lo, right, dims):
    right_hi, right_lo = split_bf16(right)
    return bf16_dot(left_hi, right_hi, dims) + bf16_dot(left_hi, right_lo, dims) + bf16_dot(left_lo, right_hi, dims)


def make_shards(n_shard, n_section, n_ts):
    rows = D // n_shard
    cols = D // n_ts
    assert rows % cols == 0 or cols % rows == 0
    pair = n_shard == 2

    def partner(x):
        return lax.ppermute(x, "shard", [(0, 1), (1, 0)])

    def shard_concat(x, c):
        if not pair:
            return lax.all_gather(x, "shard", axis=0, tiled=True)
        other = partner(x)
        first = jnp.where(c == 0, x, other)
        last = jnp.where(c == 0, other, x)
        return jnp.concatenate([first, last], axis=0)

    def shard_sum(x):
        if not pair:
            return lax.psum(x, "shard")
        return x + partner(x)

    def shard_sum_scatter(x, c, axis):
        if not pair:
            return lax.psum_scatter(x, "shard", scatter_dimension=axis, tiled=True)
        size = x.shape[axis] // 2
        mine = lax.dynamic_slice_in_dim(x, c * size, size, axis=axis)
        theirs = lax.dynamic_slice_in_dim(x, (1 - c) * size, size, axis=axis)
        return mine + partner(theirs)

    def block_rows(grad_rows, k, c):
        start = k * cols
        if cols <= rows:
            piece = lax.dynamic_slice_in_dim(grad_rows, start % rows, cols, axis=0)
            owner = start // rows
            if pair:
                return jnp.where(owner == c, piece, partner(piece))
            pieces = lax.all_gather(piece, "shard", axis=0, tiled=False)
            return lax.dynamic_index_in_dim(pieces, owner, axis=0, keepdims=False)
        full = lax.all_gather(grad_rows, "shard", axis=0, tiled=True)
        return lax.dynamic_slice_in_dim(full, start, cols, axis=0)

    def all_sum(value):
        x = jnp.full((PAD, 128), value, jnp.float32)
        if n_ts & (n_ts - 1) == 0:
            step = 1
            while step < n_ts:
                x = x + lax.ppermute(x, TS, [(i, i ^ step) for i in range(n_ts)])
                step *= 2
        else:
            x = lax.psum(x, TS)
        return shard_sum(x)[0, 0]

    def newton_step(iterate):
        iterate_rows = lax.all_gather(iterate, TS, axis=1, tiled=True)
        z_cols = shard_sum(contract_rows(iterate_rows, iterate))
        return 1.5 * iterate - 0.5 * exact_dot(iterate_rows, z_cols)

    def shards(grad_parts, moment, second, stat_left, basis_left):
        c = lax.axis_index("shard")
        k = lax.axis_index("tensor") * n_section + lax.axis_index("section")
        part = grad_parts[0]
        if pair:
            mine = lax.dynamic_slice_in_dim(part, c * rows, rows, axis=1)
            theirs = lax.dynamic_slice_in_dim(part, (1 - c) * rows, rows, axis=1)
            grad_flip = (mine.astype(jnp.float32) + partner(theirs).astype(jnp.float32)).astype(jnp.bfloat16)
        else:
            grad_flip = lax.psum_scatter(
                part.astype(jnp.float32).astype(jnp.bfloat16), "shard", scatter_dimension=1, tiled=True
            )
        grad = grad_flip.T
        grad_cols = shard_concat(grad, c)
        basis_hi, basis_lo = split_bf16(basis_left)
        stacked = lax.all_gather(jnp.stack([grad, basis_hi, basis_lo]), TS, axis=2, tiled=True)
        grad_rows, hi_rows, lo_rows = stacked[0], stacked[1], stacked[2]
        if cols <= rows and pair:
            piece = lax.dynamic_slice(stacked, (0, (k * cols) % rows, 0), (1, cols, D))[0]
            grad_krows = jnp.where((k * cols) // rows == c, piece, partner(piece))
        else:
            grad_krows = block_rows(grad_rows, k, c)
        gram = lax.dot_general(
            grad_rows, grad_krows, (((1,), (1,)), ((), ())), preferred_element_type=jnp.float32
        )
        stat_next = stat_decay * stat_left + (1.0 - stat_decay) / D * gram
        by_rows = ((1,), (0,))
        stat_hi, stat_lo = split_bf16(shard_concat(stat_next, c))
        quads = bf16_dot(stacked[1:], jnp.concatenate([stat_hi, stat_lo], axis=1), ((2,), (0,)))
        power = quads[0, :, :cols] + quads[0, :, cols:] + quads[1, :, :cols]
        hi_later, lo_later = hi_rows, lo_rows
        rotated = bf16_dot(hi_later, grad_cols, by_rows) + bf16_dot(lo_later, grad_cols, by_rows)
        moment_next = beta_one * moment + (1.0 - beta_one) * rotated
        second_next = beta_two * second + (1.0 - beta_two) * rotated * rotated
        ratio = moment_next / first_fix / (jnp.sqrt(second_next / second_fix) + adam_eps)
        update = shard_sum_scatter(split_dot(hi_later, lo_later, ratio, ((0,), (0,))), c, 0)
        power_rows = lax.all_gather(power, TS, axis=1, tiled=True)
        total_sq = all_sum(jnp.sum(power * power))
        power_rows, update, total_sq = lax.optimization_barrier((power_rows, update, total_sq))
        z_cols = shard_sum(contract_rows(power_rows, power))
        scale = shrink * jnp.sqrt(D / (total_sq + norm_eps))
        iterate = (1.5 * scale) * power - (0.5 * scale * scale * scale) * exact_dot(power_rows, z_cols)
        for turn in range(NS_ITERS - 1):
            iterate = newton_step(iterate)
        return (update, moment_next, second_next, stat_next, iterate)

    return shards


def solution(mesh):
    n_shard = mesh.shape["shard"]
    n_section = mesh.shape["section"]
    n_ts = mesh.shape["tensor"] * n_section
    in_specs = (
        P("shard", TS, None),
        P("shard", TS),
        P("shard", TS),
        P("shard", TS),
        P("shard", TS),
    )
    out_specs = (
        P("shard", TS),
        P("shard", TS),
        P("shard", TS),
        P("shard", TS),
        P("shard", TS),
    )
    return jax.shard_map(
        make_shards(n_shard, n_section, n_ts), mesh=mesh, in_specs=in_specs, out_specs=out_specs, check_vma=False
    )
```
